128 devices in a mesh: seq: 8 (over x, core), tensor: 16 (over z, y).
Axes of the slice: x: 4, y: 4, z: 4, core: 2. Of those that a mesh axis runs over, the one named last changes fastest.
Arguments:
- tokens: bfloat16 [4096, 2560], P(('seq', 'tensor')), may hold values from -6 to 6
- in_gate: bfloat16 [2560, 5120], P(None, 'tensor')
- in_x: bfloat16 [2560, 5120], P(None, 'tensor'), may hold values from -0.125 to 0.125
- in_dt: bfloat16 [2560, 80], P(None, 'tensor'), may hold values from -0.125 to 0.125
- in_bc: bfloat16 [2560, 256], replicated, may hold values from -0.125 to 0.125
- conv_x_weight: float32 [4, 5120], P(None, 'tensor'), may hold values from -3 to 3
- conv_x_bias: float32 [5120], P('tensor'), may hold values from -0.5 to 0.5
- conv_bc_weight: float32 [4, 256], replicated, may hold values from -3 to 3
- conv_bc_bias: float32 [256], replicated, may hold values from -0.5 to 0.5
- dt_bias: float32 [80], P('tensor'), may hold values from -2 to 1
- head_rate: float32 [80], P('tensor'), may hold values from 2.4414063e-05 to 0.05
- skip_gain: float32 [80], P('tensor'), may hold values from 0.5 to 1.5
- norm_gain: float32 [5120], P('tensor'), may hold values from 0.5 to 1.5
- out_weight: bfloat16 [5120, 2560], P('tensor'), may hold values from -0.078125 to 0.078125
- lengths: int32 [16], replicated, may hold values from 17 to 2048, as said below
- accepted: int32 [16], replicated, may hold values from 0 to 16
- slots: int32 [16], replicated, may hold values from 0 to 15, each once
Outputs:
- mixed: bfloat16 [4096, 2560], P(('seq', 'tensor'))
- accepted_states: float32 [16, 80, 64, 128], P('seq', 'tensor')
The draws below stay inside these ranges and needn't reach their ends.
Inputs may be any that keep to these rules, and one draw needn't show every extreme that they name: The 16 lengths sum to 4096; requests are packed in order, and the last 16 tokens of each request are its drafts. `slots`: every slot 0 to 15 is named once.
All inputs are finite; a program needn't handle non-finite values.
Results may differ from the reference program's by a relative error of at most 0.02.
Values may be sent and summed in bfloat16 or wider, within the bound.
No kernel may reach another device: no remote copies, remote signals or barrier semaphores. Data moves between devices by JAX's collectives and lax.ppermute only.
A program may use at most 64 MiB of HBM per device.

```python
import math
import jax
import jax.numpy as jnp
from jax import lax

D = 2560
HEADS = 80
HEADDIM = 64
STATE = 128
CONV = 4
BLOCK = 256
DRAFTS = 16
INNER = 5120
TOKENS = 4096
REQS = 16
N_TENSOR = 16


def draw_lengths(key, part):
    first_key = jax.random.fold_in(key, 11)
    second_key = jax.random.fold_in(key, 12)
    longest_size = TOKENS // 2
    spare = TOKENS - longest_size - (REQS - 1) * (DRAFTS + 1)
    powers = jax.random.randint(first_key, (REQS,), 0, 10)
    weights = jnp.left_shift(jnp.ones((REQS,), jnp.int32), powers)
    shortest = jax.random.randint(second_key, (), 0, REQS)
    longest = (shortest + 1) % REQS
    receiver = (shortest + 2) % REQS
    order = jnp.arange(REQS, dtype=jnp.int32)
    weights = jnp.where((order == shortest) | (order == longest), 0, weights)
    extra = spare * weights // jnp.sum(weights)
    remainder = spare - jnp.sum(extra)
    extra = extra + jnp.where(order == receiver, remainder, 0)
    sizes = DRAFTS + 1 + extra
    sizes = jnp.where(order == longest, longest_size, sizes)
    return sizes.astype(jnp.int32)


def draw_accepted(key, part):
    first_key = jax.random.fold_in(key, 21)
    second_key = jax.random.fold_in(key, 22)
    third_key = jax.random.fold_in(key, 23)
    counts = jax.random.randint(first_key, (REQS,), 0, DRAFTS + 1)
    lowest = jax.random.randint(second_key, (), 0, REQS)
    highest = (lowest + 1 + jax.random.randint(third_key, (), 0, REQS - 1)) % REQS
    order = jnp.arange(REQS, dtype=jnp.int32)
    counts = jnp.where(order == lowest, 0, counts)
    counts = jnp.where(order == highest, DRAFTS, counts)
    return counts.astype(jnp.int32)


def draw_in_gate(key, part):
    column_scale = 1.0 + 2.0 * jnp.arange(INNER, dtype=jnp.float32) / (INNER - 1)
    values = jax.random.normal(key, (D, INNER), jnp.float32)
    return (values * column_scale[None, :] / jnp.sqrt(jnp.float32(D))).astype(jnp.bfloat16)


def shard_levels(own_key, shape, pieces, least, largest):
    def one(axis_at, shards_of):
        draws = jax.random.uniform(jax.random.fold_in(jax.random.fold_in(own_key, 6), axis_at), (shards_of,), jnp.float32, least / len(pieces), largest / len(pieces))
        return jnp.repeat(jnp.exp(draws), shape[axis_at] // shards_of).reshape((-1,) + (1,) * (len(shape) - axis_at - 1))

    factor_of = one(*pieces[0])
    for cut in pieces[1:]:
        factor_of = factor_of * one(*cut)
    return factor_of


def centred(stream_key, extent, width, most, cuts=(), held_as=jnp.bfloat16):
    result = jax.random.normal(stream_key, extent, jnp.float32) * width
    if len(cuts) > 0:
        result = shard_levels(stream_key, extent, cuts, -0.22, 0.18) * result
    return jnp.clip(result, min=-most, max=most).astype(held_as)


def setup_inputs(seed: int = 0) -> dict:
    key_of = jax.random.split(jax.random.key(seed), 18)
    tokens = centred(key_of[0], (TOKENS, D), 1.0, 6.0, ((0, 128),))
    in_gate = draw_in_gate(jax.random.fold_in(key_of[17], 71), 0)
    in_x = centred(key_of[2], (D, INNER), D ** -0.5, 0.125, ((1, 16),))
    in_dt = centred(key_of[3], (D, HEADS), D ** -0.5, 0.125, ((1, 16),))
    in_bc = centred(key_of[4], (D, 2 * STATE), D ** -0.5, 0.125)
    conv_x_weight = centred(key_of[5], (CONV, INNER), CONV ** -0.5, 3.0, ((1, 16),), jnp.float32)
    conv_x_bias = jnp.clip(jax.random.uniform(key_of[6], (INNER,), jnp.float32, -0.5, 0.5) * shard_levels(key_of[6], (INNER,), ((0, 16),), -0.4, 0.0), -0.5, 0.5)
    conv_bc_weight = centred(key_of[7], (CONV, 2 * STATE), CONV ** -0.5, 3.0, (), jnp.float32)
    conv_bc_bias = jnp.clip(jax.random.uniform(key_of[8], (2 * STATE,), jnp.float32, -0.5, 0.5), -0.5, 0.5)
    dt_bias = jnp.clip(-2.0 + 3.0 * jax.random.uniform(key_of[9], (HEADS,), jnp.float32) ** shard_levels(key_of[9], (HEADS,), ((0, 16),), -0.2, 0.2), -2.0, 1.0)
    head_rate = jnp.clip(jnp.exp(math.log(0.05) - 7.624619 * jax.random.uniform(key_of[10], (HEADS,), jnp.float32) ** shard_levels(key_of[10], (HEADS,), ((0, 16),), -0.2, 0.2)), 2.441406286379788e-05, 0.05)
    skip_gain = jnp.clip(0.5 + 1.0 * jax.random.uniform(key_of[11], (HEADS,), jnp.float32) ** shard_levels(key_of[11], (HEADS,), ((0, 16),), -0.2, 0.2), 0.5, 1.5)
    norm_gain = jnp.clip(1.0 + 0.1 * jax.random.normal(key_of[12], (INNER,), jnp.float32), 0.5, 1.5)
    out_weight = centred(key_of[13], (INNER, D), INNER ** -0.5, 0.078125, ((0, 16),))
    lengths = draw_lengths(jax.random.fold_in(key_of[17], 71), 0)
    accepted = draw_accepted(jax.random.fold_in(key_of[17], 71), 0)
    slots = jax.random.permutation(key_of[16], REQS).astype(jnp.int32)
    return {"tokens": tokens, "in_gate": in_gate, "in_x": in_x, "in_dt": in_dt, "in_bc": in_bc, "conv_x_weight": conv_x_weight, "conv_x_bias": conv_x_bias, "conv_bc_weight": conv_bc_weight, "conv_bc_bias": conv_bc_bias, "dt_bias": dt_bias, "head_rate": head_rate, "skip_gain": skip_gain, "norm_gain": norm_gain, "out_weight": out_weight, "lengths": lengths, "accepted": accepted, "slots": slots}


HIGHEST_PRECISION = lax.Precision.HIGHEST

def segment_of(positions, starts):
    return (lax.optimization_barrier(jnp.sum((starts[None, :] <= positions[:, None]).astype(jnp.int32), axis=1)) - 1).astype(jnp.int32)

def reference(tokens, in_gate, in_x, in_dt, in_bc, conv_x_weight, conv_x_bias, conv_bc_weight, conv_bc_bias, dt_bias, head_rate, skip_gain, norm_gain, out_weight, lengths, accepted, slots):
    starts = (jnp.cumsum(lengths) - lengths).astype(jnp.int32)
    positions = jnp.arange(TOKENS, dtype=jnp.int32)
    segment = segment_of(positions, starts)
    before = segment_of(positions - 1, starts)
    weights = jnp.concatenate([in_gate, in_x, in_dt, in_bc], axis=1)
    conv_weight = jnp.concatenate([conv_x_weight, conv_bc_weight], axis=1)
    conv_bias = jnp.concatenate([conv_x_bias, conv_bc_bias])
    group_width = INNER // N_TENSOR
    out_groups = out_weight.astype(jnp.float32).reshape(N_TENSOR, group_width, D)
    block_total = TOKENS // BLOCK
    token_blocks = tokens.reshape(block_total, BLOCK, D)
    segment_blocks = segment.reshape(block_total, BLOCK)
    first_before = before.reshape(block_total, BLOCK)[:, 0]
    lower = jnp.arange(BLOCK)[:, None] >= jnp.arange(BLOCK)[None, :]

    def advance(carry, item):
        state, tail, tail_segment = carry
        rows_in, segs, prior = item
        projected = jnp.dot(rows_in, weights, preferred_element_type=jnp.float32)
        gate = projected[:, :INNER]
        inputs = jnp.concatenate([projected[:, INNER:2 * INNER], projected[:, 2 * INNER + HEADS:]], axis=1)
        raw_step = projected[:, 2 * INNER:2 * INNER + HEADS]
        extended = jnp.concatenate([tail, inputs], axis=0)
        extended_segment = jnp.concatenate([tail_segment, segs])
        conv = jnp.zeros_like(inputs) + conv_bias[None, :]
        for offset in range(CONV):
            match = (extended_segment[offset:offset + BLOCK] == segs).astype(jnp.float32)
            conv = conv + conv_weight[offset][None, :] * extended[offset:offset + BLOCK] * match[:, None]
        active = jax.nn.silu(conv)
        values = active[:, :INNER].reshape(BLOCK, HEADS, HEADDIM)
        keys = active[:, INNER:INNER + STATE]
        queries = active[:, INNER + STATE:]
        step_size = jax.nn.softplus(raw_step + dt_bias[None, :])
        decay_sum = jnp.cumsum(-head_rate[None, :] * step_size, axis=0)
        same = (segs[:, None] == segs[None, :]) & lower
        spread = decay_sum[:, None, :] - decay_sum[None, :, :]
        decay = jnp.where(same[:, :, None], jnp.exp(jnp.minimum(spread, 0.0)), 0.0)
        gram = jnp.dot(queries, keys.T, preferred_element_type=jnp.float32, precision=HIGHEST_PRECISION)
        mixing = gram[:, :, None] * decay * step_size[None, :, :]
        inner = jnp.einsum('ijh,jhp->ihp', mixing, values, precision=HIGHEST_PRECISION)
        keep = jnp.exp(decay_sum) * (segs == prior).astype(jnp.float32)[:, None]
        outer = keep[:, :, None] * jnp.einsum('in,hpn->ihp', queries, state, precision=HIGHEST_PRECISION)
        output = inner + outer + skip_gain[None, :, None] * values
        gated = output.reshape(BLOCK, INNER) * jax.nn.silu(gate)
        scale = lax.rsqrt(lax.optimization_barrier(jnp.mean(gated * gated, axis=1, keepdims=True)) + 1e-05)
        normed = (gated * scale * norm_gain[None, :]).astype(jnp.bfloat16)
        normed_groups = normed.astype(jnp.float32).reshape(BLOCK, N_TENSOR, group_width)
        partial_value = jnp.einsum('bgc,gcd->bgd', normed_groups, out_groups).astype(jnp.bfloat16)
        mixed = lax.optimization_barrier(jnp.sum(partial_value.astype(jnp.float32), axis=1)).astype(jnp.bfloat16)
        weight_last = jnp.exp(decay_sum[-1][None, :] - decay_sum) * step_size * (segs == segs[-1]).astype(jnp.float32)[:, None]
        local = jnp.einsum('jhp,jn->hpn', weight_last[:, :, None] * values, keys, precision=HIGHEST_PRECISION)
        passes = jnp.exp(decay_sum[-1]) * (segs[-1] == prior).astype(jnp.float32)
        new_state = passes[:, None, None] * state + local
        new_carry = (new_state, inputs[BLOCK - CONV + 1:], segs[BLOCK - CONV + 1:])
        return (new_carry, (mixed, state, values, keys, step_size, decay_sum))
    initial = (jnp.zeros((HEADS, HEADDIM, STATE), jnp.float32), jnp.zeros((CONV - 1, INNER + 2 * STATE), jnp.float32), jnp.full((CONV - 1,), -1, jnp.int32))
    _, outputs = lax.scan(advance, initial, (token_blocks, segment_blocks, first_before))
    mixed, start_states, values_all, keys_all, steps_all, sums_all = outputs
    mixed = mixed.reshape(TOKENS, D)
    ends = (starts + lengths - 1 - DRAFTS + accepted).astype(jnp.int32)
    which = (ends // BLOCK).astype(jnp.int32)
    place = (ends % BLOCK).astype(jnp.int32)

    def pick(index):
        block_id = which[index]
        spot = place[index]
        sums = sums_all[block_id]
        total = sums[spot]
        valid = (jnp.arange(BLOCK, dtype=jnp.int32) <= spot) & (segment_blocks[block_id] == index)
        weight = jnp.where(valid[:, None], jnp.exp(jnp.minimum(total[None, :] - sums, 0.0)) * steps_all[block_id], 0.0)
        part = jnp.einsum('jhp,jn->hpn', weight[:, :, None] * values_all[block_id], keys_all[block_id], precision=HIGHEST_PRECISION)
        carried = jnp.exp(total) * (first_before[block_id] == index).astype(jnp.float32)
        return carried[:, None, None] * start_states[block_id] + part
    states = lax.map(pick, jnp.arange(REQS, dtype=jnp.int32))
    accepted_states = jnp.zeros_like(states).at[slots].set(states)
    return (mixed, accepted_states)
```

```python
import jax
import jax.numpy as jnp
from jax import lax
from jax.sharding import PartitionSpec as P

BLOCK = 256
DRAFTS = 16


HIGHEST_PRECISION = lax.Precision.HIGHEST


def passed_along(block, axis, distance):
    devices = range(lax.axis_size(axis))
    route = [(i - distance, i) for i in devices if i - distance in devices]
    return lax.ppermute(block, axis, route)


def segment_of(positions, starts):
    return jnp.sum((starts[None, :] <= positions[:, None]).astype(jnp.int32), axis=1) - 1


def per_device(
    tokens,
    in_gate,
    in_x,
    in_dt,
    in_bc,
    conv_x_weight,
    conv_x_bias,
    conv_bc_weight,
    conv_bc_bias,
    dt_bias,
    head_rate,
    skip_gain,
    norm_gain,
    out_weight,
    lengths,
    accepted,
    slots,
):
    local_inner = in_x.shape[1]
    local_heads = in_dt.shape[1]
    head_size = local_inner // local_heads
    state_size = in_bc.shape[1] // 2
    tensor_count = lax.axis_size("tensor")
    seq_count = lax.axis_size("seq")
    weight_all = jnp.concatenate([in_gate, in_x, in_dt, in_bc], axis=1)
    projected = jnp.dot(
        lax.all_gather(tokens, "tensor", axis=0, tiled=True),
        weight_all,
        preferred_element_type=jnp.float32,
    )
    bc_inputs = projected[:, 2 * local_inner + local_heads :]
    gate = projected[:, :local_inner]
    raw_step = projected[:, 2 * local_inner : 2 * local_inner + local_heads]
    inputs = jnp.concatenate([projected[:, local_inner : 2 * local_inner], bc_inputs], axis=1)
    row_count = projected.shape[0]
    first = lax.axis_index("seq") * row_count
    starts = jnp.cumsum(lengths) - lengths
    segment = segment_of(first + jnp.arange(row_count, dtype=jnp.int32), starts)
    taps = conv_x_weight.shape[0]
    edge = passed_along(inputs[row_count - taps + 1 :], "seq", 1)
    edge_segment = segment_of(first - taps + 1 + jnp.arange(taps - 1, dtype=jnp.int32), starts)
    extended = jnp.concatenate([edge, inputs], axis=0)
    extended_segment = jnp.concatenate([edge_segment, segment])
    conv_weight = jnp.concatenate([conv_x_weight, conv_bc_weight], axis=1)
    conv_bias = jnp.concatenate([conv_x_bias, conv_bc_bias])
    conv = jnp.zeros_like(inputs) + conv_bias[None, :]
    for offset in range(taps):
        match = (extended_segment[offset : offset + row_count] == segment).astype(jnp.float32)
        conv = (
            conv
            + conv_weight[offset][None, :] * extended[offset : offset + row_count] * match[:, None]
        )
    active = jax.nn.silu(conv)
    block_count = row_count // BLOCK
    values = active[:, :local_inner].reshape(block_count, BLOCK, local_heads, head_size)
    keys = active[:, local_inner : local_inner + state_size].reshape(block_count, BLOCK, state_size)
    queries = active[:, local_inner + state_size :].reshape(block_count, BLOCK, state_size)
    step_size = jax.nn.softplus(raw_step + dt_bias[None, :])
    decay_sum = jnp.cumsum(
        (-head_rate[None, :] * step_size).reshape(block_count, BLOCK, local_heads), axis=1
    )
    steps = step_size.reshape(block_count, BLOCK, local_heads)
    segs = segment.reshape(block_count, BLOCK)
    prior = segment_of(first + jnp.arange(block_count, dtype=jnp.int32) * BLOCK - 1, starts)
    lower = jnp.arange(BLOCK)[:, None] >= jnp.arange(BLOCK)[None, :]
    same = (segs[:, :, None] == segs[:, None, :]) & lower[None]
    spread = decay_sum[:, :, None, :] - decay_sum[:, None, :, :]
    decay = jnp.where(same[..., None], jnp.exp(jnp.minimum(spread, 0.0)), 0.0)
    gram = jnp.einsum("cin,cjn->cij", queries, keys, precision=HIGHEST_PRECISION)
    mixing = gram[..., None] * decay * steps[:, None, :, :]
    inner = jnp.einsum("cijh,cjhp->cihp", mixing, values, precision=HIGHEST_PRECISION)
    last_match = (segs == segs[:, -1:]).astype(jnp.float32)
    weight_last = jnp.exp(decay_sum[:, -1:, :] - decay_sum) * steps * last_match[..., None]
    local = jnp.einsum(
        "cjhp,cjn->chpn", weight_last[..., None] * values, keys, precision=HIGHEST_PRECISION
    )
    passes = jnp.exp(decay_sum[:, -1, :]) * (segs[:, -1] == prior).astype(jnp.float32)[:, None]

    def advance(carry, item):
        zero_start, factor = carry
        local_state, passing = item
        return (
            (passing[:, None, None] * zero_start + local_state, passing * factor),
            (zero_start, factor),
        )

    empty = jnp.zeros((local_heads, head_size, state_size), jnp.float32)
    unit = jnp.ones((local_heads,), jnp.float32)
    (zero_end, factor_end), (zero_starts, factors) = lax.scan(
        advance, (empty, unit), (local, passes)
    )

    factor_high = factor_end.astype(jnp.bfloat16)
    factor_low = (factor_end - factor_high.astype(jnp.float32)).astype(jnp.bfloat16)
    factor_rows = jnp.zeros((local_heads, 16, state_size), jnp.bfloat16)
    factor_rows = factor_rows.at[:, 0, :].set(factor_high[:, None])
    factor_rows = factor_rows.at[:, 1, :].set(factor_low[:, None])
    sent = lax.all_gather(
        jnp.concatenate([zero_end.astype(jnp.bfloat16), factor_rows], axis=1), "seq", axis=0
    )
    sent_states = sent[:, :, :head_size]
    sent_factors = sent[:, :, head_size, 0].astype(jnp.float32) + sent[
        :, :, head_size + 1, 0
    ].astype(jnp.float32)
    seq_index = lax.axis_index("seq")
    incoming = empty
    for earlier in range(seq_count - 1):
        advanced = sent_factors[earlier][:, None, None] * incoming + sent_states[earlier].astype(
            jnp.float32
        )
        incoming = jnp.where(earlier < seq_index, advanced, incoming)
    block_states = zero_starts + factors[:, :, None, None] * incoming[None]
    keep = jnp.exp(decay_sum) * (segs == prior[:, None]).astype(jnp.float32)[..., None]
    outer = keep[..., None] * jnp.einsum(
        "cin,chpn->cihp", queries, block_states, precision=HIGHEST_PRECISION
    )
    output = (inner + outer + skip_gain[None, None, :, None] * values).reshape(
        row_count, local_inner
    )
    gated = output * jax.nn.silu(gate)
    squares = jnp.sum(gated * gated, axis=1)
    totals = lax.psum_scatter(squares, "tensor", scatter_dimension=0, tiled=True)
    unscaled = (gated * norm_gain[None, :]).astype(jnp.bfloat16)
    reduced = lax.psum_scatter(
        jnp.dot(unscaled, out_weight, preferred_element_type=jnp.float32).astype(jnp.bfloat16),
        "tensor",
        scatter_dimension=0,
        tiled=True,
    )
    scale = lax.rsqrt(totals[:, None] / (local_inner * tensor_count) + 1e-05)
    mixed = (reduced.astype(jnp.float32) * scale).astype(jnp.bfloat16)
    request_count = lengths.shape[0]
    request_ids = jnp.arange(request_count, dtype=jnp.int32)
    ends = starts + lengths - 1 - DRAFTS + accepted
    present = (ends >= first) & (ends < first + row_count)
    local_end = jnp.clip(ends - first, 0, row_count - 1)
    which = local_end // BLOCK
    place = local_end % BLOCK
    chosen_values = jnp.take(values, which, axis=0)
    chosen_keys = jnp.take(keys, which, axis=0)
    chosen_sums = jnp.take(decay_sum, which, axis=0)
    chosen_steps = jnp.take(steps, which, axis=0)
    chosen_segs = jnp.take(segs, which, axis=0)
    end_sums = chosen_sums[request_ids, place]
    valid = (jnp.arange(BLOCK, dtype=jnp.int32)[None, :] <= place[:, None]) & (
        chosen_segs == request_ids[:, None]
    )
    weight = jnp.where(
        valid[..., None],
        jnp.exp(jnp.minimum(end_sums[:, None, :] - chosen_sums, 0.0)) * chosen_steps,
        0.0,
    )
    part = jnp.einsum(
        "rjhp,rjn->rhpn",
        weight[..., None] * chosen_values,
        chosen_keys,
        precision=HIGHEST_PRECISION,
    )
    carried = (
        jnp.exp(end_sums) * (jnp.take(prior, which) == request_ids).astype(jnp.float32)[:, None]
    )
    end_states = carried[:, :, None, None] * jnp.take(block_states, which, axis=0) + part
    end_states = jnp.where(present[:, None, None, None], end_states, 0.0)
    inverse = jnp.sum(
        (slots[None, :] == request_ids[:, None]).astype(jnp.int32) * request_ids[None, :], axis=1
    )
    outgoing = jnp.take(end_states, inverse, axis=0)
    received = lax.all_to_all(
        outgoing.astype(jnp.bfloat16), "seq", split_axis=0, concat_axis=0, tiled=True
    ).astype(outgoing.dtype)
    mine = jnp.sum(
        received.reshape(seq_count, request_count // seq_count, local_heads, head_size, state_size),
        axis=0,
    )
    return (mixed, mine)


def solution(mesh):
    return jax.shard_map(
        per_device,
        mesh=mesh,
        in_specs=(
            P(("seq", "tensor"), None),
            P(None, "tensor"),
            P(None, "tensor"),
            P(None, "tensor"),
            P(),
            P(None, "tensor"),
            P("tensor"),
            P(),
            P(),
            P("tensor"),
            P("tensor"),
            P("tensor"),
            P("tensor"),
            P("tensor", None),
            P(),
            P(),
            P(),
        ),
        out_specs=(P(("seq", "tensor"), None), P("seq", "tensor", None, None)),
        check_vma=False,
    )
```

```python
import jax
import jax.numpy as jnp
from jax import lax
from jax.sharding import PartitionSpec as P

BLOCK = 256
DRAFTS = 16


HIGHEST_PRECISION = lax.Precision.HIGHEST


def passed_along(block, axis, distance):
    devices = range(lax.axis_size(axis))
    route = [(i - distance, i) for i in devices if i - distance in devices]
    return lax.ppermute(block, axis, route)


def segment_of(positions, starts):
    return jnp.sum((starts[None, :] <= positions[:, None]).astype(jnp.int32), axis=1) - 1


def per_device(
    tokens,
    in_gate,
    in_x,
    in_dt,
    in_bc,
    conv_x_weight,
    conv_x_bias,
    conv_bc_weight,
    conv_bc_bias,
    dt_bias,
    head_rate,
    skip_gain,
    norm_gain,
    out_weight,
    lengths,
    accepted,
    slots,
):
    local_inner = in_x.shape[1]
    local_heads = in_dt.shape[1]
    head_size = local_inner // local_heads
    state_size = in_bc.shape[1] // 2
    tensor_count = lax.axis_size("tensor")
    seq_count = lax.axis_size("seq")
    weight_all = jnp.concatenate([in_gate, in_x, in_dt, in_bc], axis=1)
    gathered = lax.all_to_all(
        jnp.tile(tokens, (lax.axis_size("tensor"), 1)), "tensor", 0, 0, tiled=True
    )
    projected = jnp.dot(
        gathered,
        weight_all,
        preferred_element_type=jnp.float32,
    )
    bc_inputs = projected[:, 2 * local_inner + local_heads :]
    gate = projected[:, :local_inner]
    raw_step = projected[:, 2 * local_inner : 2 * local_inner + local_heads]
    inputs = jnp.concatenate([projected[:, local_inner : 2 * local_inner], bc_inputs], axis=1)
    row_count = projected.shape[0]
    first = lax.axis_index("seq") * row_count
    starts = jnp.cumsum(lengths) - lengths
    segment = segment_of(first + jnp.arange(row_count, dtype=jnp.int32), starts)
    taps = conv_x_weight.shape[0]
    edge = passed_along(inputs[row_count - taps + 1 :], "seq", 1)
    edge_segment = segment_of(first - taps + 1 + jnp.arange(taps - 1, dtype=jnp.int32), starts)
    extended = jnp.concatenate([edge, inputs], axis=0)
    extended_segment = jnp.concatenate([edge_segment, segment])
    conv_weight = jnp.concatenate([conv_x_weight, conv_bc_weight], axis=1)
    conv_bias = jnp.concatenate([conv_x_bias, conv_bc_bias])
    conv = jnp.zeros_like(inputs) + conv_bias[None, :]
    for offset in range(taps):
        match = (extended_segment[offset : offset + row_count] == segment).astype(jnp.float32)
        conv = (
            conv
            + conv_weight[offset][None, :] * extended[offset : offset + row_count] * match[:, None]
        )
    active = jax.nn.silu(conv)
    block_count = row_count // BLOCK
    values = active[:, :local_inner].reshape(block_count, BLOCK, local_heads, head_size)
    keys = active[:, local_inner : local_inner + state_size].reshape(block_count, BLOCK, state_size)
    queries = active[:, local_inner + state_size :].reshape(block_count, BLOCK, state_size)
    step_size = jax.nn.softplus(raw_step + dt_bias[None, :])
    decay_sum = jnp.cumsum(
        (-head_rate[None, :] * step_size).reshape(block_count, BLOCK, local_heads), axis=1
    )
    steps = step_size.reshape(block_count, BLOCK, local_heads)
    segs = segment.reshape(block_count, BLOCK)
    prior = segment_of(first + jnp.arange(block_count, dtype=jnp.int32) * BLOCK - 1, starts)
    lower = jnp.arange(BLOCK)[:, None] >= jnp.arange(BLOCK)[None, :]
    same = (segs[:, :, None] == segs[:, None, :]) & lower[None]
    spread = decay_sum[:, :, None, :] - decay_sum[:, None, :, :]
    decay = jnp.where(same[..., None], jnp.exp(jnp.minimum(spread, 0.0)), 0.0)
    gram = jnp.einsum("cin,cjn->cij", queries, keys, precision=HIGHEST_PRECISION)
    mixing = gram[..., None] * decay * steps[:, None, :, :]
    inner = jnp.einsum("cijh,cjhp->cihp", mixing, values, precision=HIGHEST_PRECISION)
    last_match = (segs == segs[:, -1:]).astype(jnp.float32)
    weight_last = jnp.exp(decay_sum[:, -1:, :] - decay_sum) * steps * last_match[..., None]
    local = jnp.einsum(
        "cjhp,cjn->chpn", weight_last[..., None] * values, keys, precision=HIGHEST_PRECISION
    )
    passes = jnp.exp(decay_sum[:, -1, :]) * (segs[:, -1] == prior).astype(jnp.float32)[:, None]

    def advance(carry, item):
        zero_start, factor = carry
        local_state, passing = item
        return (
            (passing[:, None, None] * zero_start + local_state, passing * factor),
            (zero_start, factor),
        )

    empty = jnp.zeros((local_heads, head_size, state_size), jnp.float32)
    unit = jnp.ones((local_heads,), jnp.float32)
    (zero_end, factor_end), (zero_starts, factors) = lax.scan(
        advance, (empty, unit), (local, passes)
    )

    factor_high = factor_end.astype(jnp.bfloat16)
    factor_low = (factor_end - factor_high.astype(jnp.float32)).astype(jnp.bfloat16)
    factor_rows = jnp.zeros((local_heads, 16, state_size), jnp.bfloat16)
    factor_rows = factor_rows.at[:, 0, :].set(factor_high[:, None])
    factor_rows = factor_rows.at[:, 1, :].set(factor_low[:, None])
    sent = lax.all_gather(
        jnp.concatenate([zero_end.astype(jnp.bfloat16), factor_rows], axis=1), "seq", axis=0
    )
    sent_states = sent[:, :, :head_size]
    sent_factors = sent[:, :, head_size, 0].astype(jnp.float32) + sent[
        :, :, head_size + 1, 0
    ].astype(jnp.float32)
    seq_index = lax.axis_index("seq")
    incoming = empty
    for earlier in range(seq_count - 1):
        advanced = sent_factors[earlier][:, None, None] * incoming + sent_states[earlier].astype(
            jnp.float32
        )
        incoming = jnp.where(earlier < seq_index, advanced, incoming)
    block_states = zero_starts + factors[:, :, None, None] * incoming[None]
    keep = jnp.exp(decay_sum) * (segs == prior[:, None]).astype(jnp.float32)[..., None]
    outer = keep[..., None] * jnp.einsum(
        "cin,chpn->cihp", queries, block_states, precision=HIGHEST_PRECISION
    )
    output = (inner + outer + skip_gain[None, None, :, None] * values).reshape(
        row_count, local_inner
    )
    gated = output * jax.nn.silu(gate)
    squares = jnp.sum(gated * gated, axis=1)
    totals = jnp.sum(
        lax.all_to_all(squares, "tensor", 0, 0, tiled=True).reshape(tensor_count, -1), axis=0
    )
    unscaled = (gated * norm_gain[None, :]).astype(jnp.bfloat16)
    partials = jnp.dot(unscaled, out_weight, preferred_element_type=jnp.float32).astype(
        jnp.bfloat16
    )
    received_partials = lax.all_to_all(partials, "tensor", 0, 0, tiled=True)
    reduced = jnp.sum(
        received_partials.reshape(tensor_count, -1, partials.shape[1]).astype(jnp.float32), axis=0
    )
    scale = lax.rsqrt(totals[:, None] / (local_inner * tensor_count) + 1e-05)
    mixed = (reduced * scale).astype(jnp.bfloat16)
    request_count = lengths.shape[0]
    request_ids = jnp.arange(request_count, dtype=jnp.int32)
    ends = starts + lengths - 1 - DRAFTS + accepted
    present = (ends >= first) & (ends < first + row_count)
    local_end = jnp.clip(ends - first, 0, row_count - 1)
    which = local_end // BLOCK
    place = local_end % BLOCK
    chosen_values = jnp.take(values, which, axis=0)
    chosen_keys = jnp.take(keys, which, axis=0)
    chosen_sums = jnp.take(decay_sum, which, axis=0)
    chosen_steps = jnp.take(steps, which, axis=0)
    chosen_segs = jnp.take(segs, which, axis=0)
    end_sums = chosen_sums[request_ids, place]
    valid = (jnp.arange(BLOCK, dtype=jnp.int32)[None, :] <= place[:, None]) & (
        chosen_segs == request_ids[:, None]
    )
    weight = jnp.where(
        valid[..., None],
        jnp.exp(jnp.minimum(end_sums[:, None, :] - chosen_sums, 0.0)) * chosen_steps,
        0.0,
    )
    part = jnp.einsum(
        "rjhp,rjn->rhpn",
        weight[..., None] * chosen_values,
        chosen_keys,
        precision=HIGHEST_PRECISION,
    )
    carried = (
        jnp.exp(end_sums) * (jnp.take(prior, which) == request_ids).astype(jnp.float32)[:, None]
    )
    end_states = carried[:, :, None, None] * jnp.take(block_states, which, axis=0) + part
    end_states = jnp.where(present[:, None, None, None], end_states, 0.0)
    inverse = jnp.sum(
        (slots[None, :] == request_ids[:, None]).astype(jnp.int32) * request_ids[None, :], axis=1
    )
    outgoing = jnp.take(end_states, inverse, axis=0)
    received = lax.all_to_all(
        outgoing.astype(jnp.bfloat16), "seq", split_axis=0, concat_axis=0, tiled=True
    ).astype(outgoing.dtype)
    mine = jnp.sum(
        received.reshape(seq_count, request_count // seq_count, local_heads, head_size, state_size),
        axis=0,
    )
    return (mixed, mine)


def solution(mesh):
    return jax.shard_map(
        per_device,
        mesh=mesh,
        in_specs=(
            P(("seq", "tensor"), None),
            P(None, "tensor"),
            P(None, "tensor"),
            P(None, "tensor"),
            P(),
            P(None, "tensor"),
            P("tensor"),
            P(),
            P(),
            P("tensor"),
            P("tensor"),
            P("tensor"),
            P("tensor"),
            P("tensor", None),
            P(),
            P(),
            P(),
        ),
        out_specs=(P(("seq", "tensor"), None), P("seq", "tensor", None, None)),
        check_vma=False,
    )
```

```python
import jax
import jax.numpy as jnp
from jax import lax
from jax.sharding import PartitionSpec as P

BLOCK = 256
DRAFTS = 16


HIGHEST_PRECISION = lax.Precision.HIGHEST


def passed_along(block, axis, distance):
    devices = range(lax.axis_size(axis))
    route = [(i - distance, i) for i in devices if i - distance in devices]
    return lax.ppermute(block, axis, route)


def segment_of(positions, starts):
    return jnp.sum((starts[None, :] <= positions[:, None]).astype(jnp.int32), axis=1) - 1


def per_device(
    tokens,
    in_gate,
    in_x,
    in_dt,
    in_bc,
    conv_x_weight,
    conv_x_bias,
    conv_bc_weight,
    conv_bc_bias,
    dt_bias,
    head_rate,
    skip_gain,
    norm_gain,
    out_weight,
    lengths,
    accepted,
    slots,
):
    local_inner = in_x.shape[1]
    local_heads = in_dt.shape[1]
    head_size = local_inner // local_heads
    state_size = in_bc.shape[1] // 2
    tensor_count = lax.axis_size("tensor")
    seq_count = lax.axis_size("seq")
    weight_all = jnp.concatenate([in_gate, in_x, in_dt, in_bc], axis=1)
    gathered = lax.all_to_all(
        jnp.tile(tokens, (lax.axis_size("tensor"), 1)), "tensor", 0, 0, tiled=True
    )
    projected = jnp.dot(
        gathered,
        weight_all,
        preferred_element_type=jnp.float32,
    )
    bc_inputs = projected[:, 2 * local_inner + local_heads :]
    gate = projected[:, :local_inner]
    raw_step = projected[:, 2 * local_inner : 2 * local_inner + local_heads]
    inputs = jnp.concatenate([projected[:, local_inner : 2 * local_inner], bc_inputs], axis=1)
    row_count = projected.shape[0]
    first = lax.axis_index("seq") * row_count
    starts = jnp.cumsum(lengths) - lengths
    segment = segment_of(first + jnp.arange(row_count, dtype=jnp.int32), starts)
    taps = conv_x_weight.shape[0]
    edge = passed_along(inputs[row_count - taps + 1 :], "seq", 1)
    edge_segment = segment_of(first - taps + 1 + jnp.arange(taps - 1, dtype=jnp.int32), starts)
    extended = jnp.concatenate([edge, inputs], axis=0)
    extended_segment = jnp.concatenate([edge_segment, segment])
    conv_weight = jnp.concatenate([conv_x_weight, conv_bc_weight], axis=1)
    conv_bias = jnp.concatenate([conv_x_bias, conv_bc_bias])
    conv = jnp.zeros_like(inputs) + conv_bias[None, :]
    for offset in range(taps):
        match = (extended_segment[offset : offset + row_count] == segment).astype(jnp.float32)
        conv = (
            conv
            + conv_weight[offset][None, :] * extended[offset : offset + row_count] * match[:, None]
        )
    active = jax.nn.silu(conv)
    block_count = row_count // BLOCK
    values = active[:, :local_inner].reshape(block_count, BLOCK, local_heads, head_size)
    keys = active[:, local_inner : local_inner + state_size].reshape(block_count, BLOCK, state_size)
    queries = active[:, local_inner + state_size :].reshape(block_count, BLOCK, state_size)
    step_size = jax.nn.softplus(raw_step + dt_bias[None, :])
    decay_sum = jnp.cumsum(
        (-head_rate[None, :] * step_size).reshape(block_count, BLOCK, local_heads), axis=1
    )
    steps = step_size.reshape(block_count, BLOCK, local_heads)
    segs = segment.reshape(block_count, BLOCK)
    prior = segment_of(first + jnp.arange(block_count, dtype=jnp.int32) * BLOCK - 1, starts)
    lower = jnp.arange(BLOCK)[:, None] >= jnp.arange(BLOCK)[None, :]
    same = (segs[:, :, None] == segs[:, None, :]) & lower[None]
    spread = decay_sum[:, :, None, :] - decay_sum[:, None, :, :]
    decay = jnp.where(same[..., None], jnp.exp(jnp.minimum(spread, 0.0)), 0.0)
    gram = jnp.einsum("cin,cjn->cij", queries, keys, precision=HIGHEST_PRECISION)
    mixing = gram[..., None] * decay * steps[:, None, :, :]
    inner = jnp.einsum("cijh,cjhp->cihp", mixing, values, precision=HIGHEST_PRECISION)
    last_match = (segs == segs[:, -1:]).astype(jnp.float32)
    weight_last = jnp.exp(decay_sum[:, -1:, :] - decay_sum) * steps * last_match[..., None]
    local = jnp.einsum(
        "cjhp,cjn->chpn", weight_last[..., None] * values, keys, precision=HIGHEST_PRECISION
    )
    passes = jnp.exp(decay_sum[:, -1, :]) * (segs[:, -1] == prior).astype(jnp.float32)[:, None]

    def advance(carry, item):
        zero_start, factor = carry
        local_state, passing = item
        return (
            (passing[:, None, None] * zero_start + local_state, passing * factor),
            (zero_start, factor),
        )

    empty = jnp.zeros((local_heads, head_size, state_size), jnp.float32)
    unit = jnp.ones((local_heads,), jnp.float32)
    (zero_end, factor_end), (zero_starts, factors) = lax.scan(
        advance, (empty, unit), (local, passes)
    )

    factor_high = factor_end.astype(jnp.bfloat16)
    factor_low = (factor_end - factor_high.astype(jnp.float32)).astype(jnp.bfloat16)
    factor_rows = jnp.zeros((local_heads, 16, state_size), jnp.bfloat16)
    factor_rows = factor_rows.at[:, 0, :].set(factor_high[:, None])
    factor_rows = factor_rows.at[:, 1, :].set(factor_low[:, None])
    packed = jnp.concatenate([zero_end.astype(jnp.bfloat16), factor_rows], axis=1)
    sent = lax.all_to_all(jnp.tile(packed[None], (seq_count, 1, 1, 1)), "seq", 0, 0, tiled=True)
    sent_states = sent[:, :, :head_size]
    sent_factors = sent[:, :, head_size, 0].astype(jnp.float32) + sent[
        :, :, head_size + 1, 0
    ].astype(jnp.float32)
    seq_index = lax.axis_index("seq")
    incoming = empty
    for earlier in range(seq_count - 1):
        advanced = sent_factors[earlier][:, None, None] * incoming + sent_states[earlier].astype(
            jnp.float32
        )
        incoming = jnp.where(earlier < seq_index, advanced, incoming)
    block_states = zero_starts + factors[:, :, None, None] * incoming[None]
    keep = jnp.exp(decay_sum) * (segs == prior[:, None]).astype(jnp.float32)[..., None]
    outer = keep[..., None] * jnp.einsum(
        "cin,chpn->cihp", queries, block_states, precision=HIGHEST_PRECISION
    )
    output = (inner + outer + skip_gain[None, None, :, None] * values).reshape(
        row_count, local_inner
    )
    gated = output * jax.nn.silu(gate)
    squares = jnp.sum(gated * gated, axis=1)
    unscaled = (gated * norm_gain[None, :]).astype(jnp.bfloat16)
    partials = jnp.dot(unscaled, out_weight, preferred_element_type=jnp.float32).astype(
        jnp.bfloat16
    )
    squares_high = squares.astype(jnp.bfloat16)
    squares_low = (squares - squares_high.astype(jnp.float32)).astype(jnp.bfloat16)
    square_columns = jnp.zeros((row_count, 128), jnp.bfloat16)
    square_columns = square_columns.at[:, 0].set(squares_high).at[:, 1].set(squares_low)
    width = partials.shape[1]
    received_partials = lax.all_to_all(
        jnp.concatenate([partials, square_columns], axis=1), "tensor", 0, 0, tiled=True
    ).reshape(tensor_count, -1, width + 128)
    reduced = jnp.sum(received_partials[:, :, :width].astype(jnp.float32), axis=0)
    totals = jnp.sum(
        received_partials[:, :, width].astype(jnp.float32)
        + received_partials[:, :, width + 1].astype(jnp.float32),
        axis=0,
    )
    scale = lax.rsqrt(totals[:, None] / (local_inner * tensor_count) + 1e-05)
    mixed = (reduced * scale).astype(jnp.bfloat16)
    request_count = lengths.shape[0]
    request_ids = jnp.arange(request_count, dtype=jnp.int32)
    ends = starts + lengths - 1 - DRAFTS + accepted
    present = (ends >= first) & (ends < first + row_count)
    local_end = jnp.clip(ends - first, 0, row_count - 1)
    which = local_end // BLOCK
    place = local_end % BLOCK
    chosen_values = jnp.take(values, which, axis=0)
    chosen_keys = jnp.take(keys, which, axis=0)
    chosen_sums = jnp.take(decay_sum, which, axis=0)
    chosen_steps = jnp.take(steps, which, axis=0)
    chosen_segs = jnp.take(segs, which, axis=0)
    end_sums = chosen_sums[request_ids, place]
    valid = (jnp.arange(BLOCK, dtype=jnp.int32)[None, :] <= place[:, None]) & (
        chosen_segs == request_ids[:, None]
    )
    weight = jnp.where(
        valid[..., None],
        jnp.exp(jnp.minimum(end_sums[:, None, :] - chosen_sums, 0.0)) * chosen_steps,
        0.0,
    )
    part = jnp.einsum(
        "rjhp,rjn->rhpn",
        weight[..., None] * chosen_values,
        chosen_keys,
        precision=HIGHEST_PRECISION,
    )
    carried = (
        jnp.exp(end_sums) * (jnp.take(prior, which) == request_ids).astype(jnp.float32)[:, None]
    )
    bracket = carried[:, :, None, None] * jnp.take(zero_starts, which, axis=0) + part
    coefficient = carried * jnp.take(factors, which, axis=0)
    end_states = bracket + coefficient[:, :, None, None] * incoming[None]
    end_states = jnp.where(present[:, None, None, None], end_states, 0.0)
    inverse = jnp.sum(
        (slots[None, :] == request_ids[:, None]).astype(jnp.int32) * request_ids[None, :], axis=1
    )
    outgoing = jnp.take(end_states, inverse, axis=0)
    received = lax.all_to_all(
        outgoing.astype(jnp.bfloat16), "seq", split_axis=0, concat_axis=0, tiled=True
    ).astype(outgoing.dtype)
    mine = jnp.sum(
        received.reshape(seq_count, request_count // seq_count, local_heads, head_size, state_size),
        axis=0,
    )
    return (mixed, mine)


def solution(mesh):
    return jax.shard_map(
        per_device,
        mesh=mesh,
        in_specs=(
            P(("seq", "tensor"), None),
            P(None, "tensor"),
            P(None, "tensor"),
            P(None, "tensor"),
            P(),
            P(None, "tensor"),
            P("tensor"),
            P(),
            P(),
            P("tensor"),
            P("tensor"),
            P("tensor"),
            P("tensor"),
            P("tensor", None),
            P(),
            P(),
            P(),
        ),
        out_specs=(P(("seq", "tensor"), None), P("seq", "tensor", None, None)),
        check_vma=False,
    )
```

```python
import jax
import jax.numpy as jnp
from jax import lax
from jax.sharding import PartitionSpec as P

BLOCK = 256
DRAFTS = 16


HIGHEST_PRECISION = lax.Precision.HIGHEST


def passed_along(block, axis, distance):
    devices = range(lax.axis_size(axis))
    route = [(i - distance, i) for i in devices if i - distance in devices]
    return lax.ppermute(block, axis, route)


def segment_of(positions, starts):
    return jnp.sum((starts[None, :] <= positions[:, None]).astype(jnp.int32), axis=1) - 1


def per_device(
    tokens,
    in_gate,
    in_x,
    in_dt,
    in_bc,
    conv_x_weight,
    conv_x_bias,
    conv_bc_weight,
    conv_bc_bias,
    dt_bias,
    head_rate,
    skip_gain,
    norm_gain,
    out_weight,
    lengths,
    accepted,
    slots,
):
    local_inner = in_x.shape[1]
    local_heads = in_dt.shape[1]
    head_size = local_inner // local_heads
    state_size = in_bc.shape[1] // 2
    tensor_count = lax.axis_size("tensor")
    seq_count = lax.axis_size("seq")
    weight_all = jnp.concatenate([in_gate, in_x, in_dt, in_bc], axis=1)
    gathered = lax.all_to_all(
        jnp.tile(tokens, (lax.axis_size("tensor"), 1)), "tensor", 0, 0, tiled=True
    )
    projected = jnp.dot(
        gathered,
        weight_all,
        preferred_element_type=jnp.float32,
    )
    bc_inputs = projected[:, 2 * local_inner + local_heads :]
    gate = projected[:, :local_inner]
    raw_step = projected[:, 2 * local_inner : 2 * local_inner + local_heads]
    inputs = jnp.concatenate([projected[:, local_inner : 2 * local_inner], bc_inputs], axis=1)
    row_count = projected.shape[0]
    first = lax.axis_index("seq") * row_count
    starts = jnp.cumsum(lengths) - lengths
    segment = segment_of(first + jnp.arange(row_count, dtype=jnp.int32), starts)
    taps = conv_x_weight.shape[0]
    edge = passed_along(inputs[row_count - taps + 1 :], "seq", 1)
    edge_segment = segment_of(first - taps + 1 + jnp.arange(taps - 1, dtype=jnp.int32), starts)
    extended = jnp.concatenate([edge, inputs], axis=0)
    extended_segment = jnp.concatenate([edge_segment, segment])
    conv_weight = jnp.concatenate([conv_x_weight, conv_bc_weight], axis=1)
    conv_bias = jnp.concatenate([conv_x_bias, conv_bc_bias])
    conv = jnp.zeros_like(inputs) + conv_bias[None, :]
    for offset in range(taps):
        match = (extended_segment[offset : offset + row_count] == segment).astype(jnp.float32)
        conv = (
            conv
            + conv_weight[offset][None, :] * extended[offset : offset + row_count] * match[:, None]
        )
    active = jax.nn.silu(conv)
    block_count = row_count // BLOCK
    values = active[:, :local_inner].reshape(block_count, BLOCK, local_heads, head_size)
    keys = active[:, local_inner : local_inner + state_size].reshape(block_count, BLOCK, state_size)
    queries = active[:, local_inner + state_size :].reshape(block_count, BLOCK, state_size)
    step_size = jax.nn.softplus(raw_step + dt_bias[None, :])
    decay_sum = jnp.cumsum(
        (-head_rate[None, :] * step_size).reshape(block_count, BLOCK, local_heads), axis=1
    )
    steps = step_size.reshape(block_count, BLOCK, local_heads)
    segs = segment.reshape(block_count, BLOCK)
    prior = segment_of(first + jnp.arange(block_count, dtype=jnp.int32) * BLOCK - 1, starts)
    lower = jnp.arange(BLOCK)[:, None] >= jnp.arange(BLOCK)[None, :]
    same = (segs[:, :, None] == segs[:, None, :]) & lower[None]
    spread = decay_sum[:, :, None, :] - decay_sum[:, None, :, :]
    decay = jnp.where(same[..., None], jnp.exp(jnp.minimum(spread, 0.0)), 0.0)
    gram = jnp.einsum("cin,cjn->cij", queries, keys, precision=HIGHEST_PRECISION)
    mixing = gram[..., None] * decay * steps[:, None, :, :]
    inner = jnp.einsum("cijh,cjhp->cihp", mixing, values, precision=HIGHEST_PRECISION)
    last_match = (segs == segs[:, -1:]).astype(jnp.float32)
    weight_last = jnp.exp(decay_sum[:, -1:, :] - decay_sum) * steps * last_match[..., None]
    local = jnp.einsum(
        "cjhp,cjn->chpn", weight_last[..., None] * values, keys, precision=HIGHEST_PRECISION
    )
    passes = jnp.exp(decay_sum[:, -1, :]) * (segs[:, -1] == prior).astype(jnp.float32)[:, None]

    def advance(carry, item):
        zero_start, factor = carry
        local_state, passing = item
        return (
            (passing[:, None, None] * zero_start + local_state, passing * factor),
            (zero_start, factor),
        )

    empty = jnp.zeros((local_heads, head_size, state_size), jnp.float32)
    unit = jnp.ones((local_heads,), jnp.float32)
    (zero_end, factor_end), (zero_starts, factors) = lax.scan(
        advance, (empty, unit), (local, passes)
    )

    factor_high = factor_end.astype(jnp.bfloat16)
    factor_low = (factor_end - factor_high.astype(jnp.float32)).astype(jnp.bfloat16)
    factor_rows = jnp.zeros((local_heads, 16, state_size), jnp.bfloat16)
    factor_rows = factor_rows.at[:, 0, :].set(factor_high[:, None])
    factor_rows = factor_rows.at[:, 1, :].set(factor_low[:, None])
    packed = jnp.concatenate([zero_end.astype(jnp.bfloat16), factor_rows], axis=1)
    sent = lax.all_to_all(jnp.tile(packed[None], (seq_count, 1, 1, 1)), "seq", 0, 0, tiled=True)
    sent_states = sent[:, :, :head_size]
    sent_factors = sent[:, :, head_size, 0].astype(jnp.float32) + sent[
        :, :, head_size + 1, 0
    ].astype(jnp.float32)
    seq_index = lax.axis_index("seq")
    incoming = empty
    for earlier in range(seq_count - 1):
        advanced = sent_factors[earlier][:, None, None] * incoming + sent_states[earlier].astype(
            jnp.float32
        )
        incoming = jnp.where(earlier < seq_index, advanced, incoming)
    block_states = zero_starts + factors[:, :, None, None] * incoming[None]
    keep = jnp.exp(decay_sum) * (segs == prior[:, None]).astype(jnp.float32)[..., None]
    outer = keep[..., None] * jnp.einsum(
        "cin,chpn->cihp", queries, block_states, precision=HIGHEST_PRECISION
    )
    output = (inner + outer + skip_gain[None, None, :, None] * values).reshape(
        row_count, local_inner
    )
    gated = output * jax.nn.silu(gate)
    squares = jnp.sum(gated * gated, axis=1)
    unscaled = (gated * norm_gain[None, :]).astype(jnp.bfloat16)
    partials = jnp.dot(unscaled, out_weight, preferred_element_type=jnp.float32).astype(
        jnp.bfloat16
    )
    squares_high = squares.astype(jnp.bfloat16)
    squares_low = (squares - squares_high.astype(jnp.float32)).astype(jnp.bfloat16)
    square_columns = jnp.zeros((row_count, 128), jnp.bfloat16)
    square_columns = square_columns.at[:, 0].set(squares_high).at[:, 1].set(squares_low)
    width = partials.shape[1]
    received_partials = lax.all_to_all(
        jnp.concatenate([partials, square_columns], axis=1), "tensor", 0, 0, tiled=True
    ).reshape(tensor_count, -1, width + 128)
    reduced = jnp.sum(received_partials[:, :, :width].astype(jnp.float32), axis=0)
    totals = jnp.sum(
        received_partials[:, :, width].astype(jnp.float32)
        + received_partials[:, :, width + 1].astype(jnp.float32),
        axis=0,
    )
    scale = lax.rsqrt(totals[:, None] / (local_inner * tensor_count) + 1e-05)
    mixed = (reduced * scale).astype(jnp.bfloat16)
    request_count = lengths.shape[0]
    request_ids = jnp.arange(request_count, dtype=jnp.int32)
    ends = starts + lengths - 1 - DRAFTS + accepted
    present = (ends >= first) & (ends < first + row_count)
    local_end = jnp.clip(ends - first, 0, row_count - 1)
    which = local_end // BLOCK
    place = local_end % BLOCK
    chosen_values = jnp.take(values, which, axis=0)
    chosen_keys = jnp.take(keys, which, axis=0)
    chosen_sums = jnp.take(decay_sum, which, axis=0)
    chosen_steps = jnp.take(steps, which, axis=0)
    chosen_segs = jnp.take(segs, which, axis=0)
    end_sums = chosen_sums[request_ids, place]
    valid = (jnp.arange(BLOCK, dtype=jnp.int32)[None, :] <= place[:, None]) & (
        chosen_segs == request_ids[:, None]
    )
    weight = jnp.where(
        valid[..., None],
        jnp.exp(jnp.minimum(end_sums[:, None, :] - chosen_sums, 0.0)) * chosen_steps,
        0.0,
    )
    part = jnp.einsum(
        "rjhp,rjn->rhpn",
        weight[..., None] * chosen_values,
        chosen_keys,
        precision=HIGHEST_PRECISION,
    )
    carried = (
        jnp.exp(end_sums) * (jnp.take(prior, which) == request_ids).astype(jnp.float32)[:, None]
    )
    bracket = carried[:, :, None, None] * jnp.take(zero_starts, which, axis=0) + part
    coefficient = carried * jnp.take(factors, which, axis=0)
    end_states = bracket + coefficient[:, :, None, None] * incoming[None]
    end_states = jnp.where(present[:, None, None, None], end_states, 0.0)
    inverse = jnp.sum(
        (slots[None, :] == request_ids[:, None]).astype(jnp.int32) * request_ids[None, :], axis=1
    )
    outgoing = jnp.take(end_states, inverse, axis=0)
    chunks = outgoing.astype(jnp.bfloat16).reshape(
        seq_count, request_count // seq_count, local_heads, head_size, state_size
    )
    pieces = [jnp.take(chunks, seq_index, axis=0).astype(jnp.float32)]
    for distance in range(1, seq_count):
        target = (seq_index + distance) % seq_count
        route = [(i, (i + distance) % seq_count) for i in range(seq_count)]
        pieces.append(
            lax.ppermute(jnp.take(chunks, target, axis=0), "seq", route).astype(jnp.float32)
        )
    mine = sum(pieces[1:], pieces[0])
    return (mixed, mine)


def solution(mesh):
    return jax.shard_map(
        per_device,
        mesh=mesh,
        in_specs=(
            P(("seq", "tensor"), None),
            P(None, "tensor"),
            P(None, "tensor"),
            P(None, "tensor"),
            P(),
            P(None, "tensor"),
            P("tensor"),
            P(),
            P(),
            P("tensor"),
            P("tensor"),
            P("tensor"),
            P("tensor"),
            P("tensor", None),
            P(),
            P(),
            P(),
        ),
        out_specs=(P(("seq", "tensor"), None), P("seq", "tensor", None, None)),
        check_vma=False,
    )
```

```python
import jax
import jax.numpy as jnp
from jax import lax
from jax.sharding import PartitionSpec as P

BLOCK = 256
DRAFTS = 16


HIGHEST_PRECISION = lax.Precision.HIGHEST


def passed_along(block, axis, distance):
    devices = range(lax.axis_size(axis))
    route = [(i - distance, i) for i in devices if i - distance in devices]
    return lax.ppermute(block, axis, route)


def segment_of(positions, starts):
    return jnp.sum((starts[None, :] <= positions[:, None]).astype(jnp.int32), axis=1) - 1


def per_device(
    tokens,
    in_gate,
    in_x,
    in_dt,
    in_bc,
    conv_x_weight,
    conv_x_bias,
    conv_bc_weight,
    conv_bc_bias,
    dt_bias,
    head_rate,
    skip_gain,
    norm_gain,
    out_weight,
    lengths,
    accepted,
    slots,
):
    local_inner = in_x.shape[1]
    local_heads = in_dt.shape[1]
    head_size = local_inner // local_heads
    state_size = in_bc.shape[1] // 2
    tensor_count = lax.axis_size("tensor")
    seq_count = lax.axis_size("seq")
    weight_all = jnp.concatenate([in_gate, in_x, in_dt, in_bc], axis=1)
    gathered = lax.all_to_all(
        jnp.tile(tokens, (lax.axis_size("tensor"), 1)), "tensor", 0, 0, tiled=True
    )
    projected = jnp.dot(
        gathered,
        weight_all,
        preferred_element_type=jnp.float32,
    )
    bc_inputs = projected[:, 2 * local_inner + local_heads :]
    gate = projected[:, :local_inner]
    raw_step = projected[:, 2 * local_inner : 2 * local_inner + local_heads]
    inputs = jnp.concatenate([projected[:, local_inner : 2 * local_inner], bc_inputs], axis=1)
    row_count = projected.shape[0]
    first = lax.axis_index("seq") * row_count
    starts = jnp.cumsum(lengths) - lengths
    segment = segment_of(first + jnp.arange(row_count, dtype=jnp.int32), starts)
    taps = conv_x_weight.shape[0]
    edge = passed_along(inputs[row_count - taps + 1 :], "seq", 1)
    edge_segment = segment_of(first - taps + 1 + jnp.arange(taps - 1, dtype=jnp.int32), starts)
    extended = jnp.concatenate([edge, inputs], axis=0)
    extended_segment = jnp.concatenate([edge_segment, segment])
    conv_weight = jnp.concatenate([conv_x_weight, conv_bc_weight], axis=1)
    conv_bias = jnp.concatenate([conv_x_bias, conv_bc_bias])
    conv = jnp.zeros_like(inputs) + conv_bias[None, :]
    for offset in range(taps):
        match = (extended_segment[offset : offset + row_count] == segment).astype(jnp.float32)
        conv = (
            conv
            + conv_weight[offset][None, :] * extended[offset : offset + row_count] * match[:, None]
        )
    active = jax.nn.silu(conv)
    block_count = row_count // BLOCK
    values = active[:, :local_inner].reshape(block_count, BLOCK, local_heads, head_size)
    keys = active[:, local_inner : local_inner + state_size].reshape(block_count, BLOCK, state_size)
    queries = active[:, local_inner + state_size :].reshape(block_count, BLOCK, state_size)
    step_size = jax.nn.softplus(raw_step + dt_bias[None, :])
    decay_sum = jnp.cumsum(
        (-head_rate[None, :] * step_size).reshape(block_count, BLOCK, local_heads), axis=1
    )
    steps = step_size.reshape(block_count, BLOCK, local_heads)
    segs = segment.reshape(block_count, BLOCK)
    prior = segment_of(first + jnp.arange(block_count, dtype=jnp.int32) * BLOCK - 1, starts)
    lower = jnp.arange(BLOCK)[:, None] >= jnp.arange(BLOCK)[None, :]
    same = (segs[:, :, None] == segs[:, None, :]) & lower[None]
    spread = decay_sum[:, :, None, :] - decay_sum[:, None, :, :]
    decay = jnp.where(same[..., None], jnp.exp(jnp.minimum(spread, 0.0)), 0.0)
    gram = jnp.einsum("cin,cjn->cij", queries, keys, precision=HIGHEST_PRECISION)
    mixing = gram[..., None] * decay * steps[:, None, :, :]
    inner = jnp.einsum("cijh,cjhp->cihp", mixing, values, precision=HIGHEST_PRECISION)
    last_match = (segs == segs[:, -1:]).astype(jnp.float32)
    weight_last = jnp.exp(decay_sum[:, -1:, :] - decay_sum) * steps * last_match[..., None]
    local = jnp.einsum(
        "cjhp,cjn->chpn", weight_last[..., None] * values, keys, precision=HIGHEST_PRECISION
    )
    passes = jnp.exp(decay_sum[:, -1, :]) * (segs[:, -1] == prior).astype(jnp.float32)[:, None]

    def advance(carry, item):
        zero_start, factor = carry
        local_state, passing = item
        return (
            (passing[:, None, None] * zero_start + local_state, passing * factor),
            (zero_start, factor),
        )

    empty = jnp.zeros((local_heads, head_size, state_size), jnp.float32)
    unit = jnp.ones((local_heads,), jnp.float32)
    (zero_end, factor_end), (zero_starts, factors) = lax.scan(
        advance, (empty, unit), (local, passes)
    )

    factor_high = factor_end.astype(jnp.bfloat16)
    factor_low = (factor_end - factor_high.astype(jnp.float32)).astype(jnp.bfloat16)
    factor_rows = jnp.zeros((local_heads, 16, state_size), jnp.bfloat16)
    factor_rows = factor_rows.at[:, 0, :].set(factor_high[:, None])
    factor_rows = factor_rows.at[:, 1, :].set(factor_low[:, None])
    packed = jnp.concatenate([zero_end.astype(jnp.bfloat16), factor_rows], axis=1)
    sent = lax.all_to_all(jnp.tile(packed[None], (seq_count, 1, 1, 1)), "seq", 0, 0, tiled=True)
    sent_states = sent[:, :, :head_size]
    sent_factors = sent[:, :, head_size, 0].astype(jnp.float32) + sent[
        :, :, head_size + 1, 0
    ].astype(jnp.float32)
    seq_index = lax.axis_index("seq")
    incoming = empty
    for earlier in range(seq_count - 1):
        advanced = sent_factors[earlier][:, None, None] * incoming + sent_states[earlier].astype(
            jnp.float32
        )
        incoming = jnp.where(earlier < seq_index, advanced, incoming)
    block_states = zero_starts + factors[:, :, None, None] * incoming[None]
    keep = jnp.exp(decay_sum) * (segs == prior[:, None]).astype(jnp.float32)[..., None]
    outer = keep[..., None] * jnp.einsum(
        "cin,chpn->cihp", queries, block_states, precision=HIGHEST_PRECISION
    )
    output = (inner + outer + skip_gain[None, None, :, None] * values).reshape(
        row_count, local_inner
    )
    gated = output * jax.nn.silu(gate)
    squares = jnp.sum(gated * gated, axis=1)
    unscaled = (gated * norm_gain[None, :]).astype(jnp.bfloat16)
    partials = jnp.dot(unscaled, out_weight, preferred_element_type=jnp.float32).astype(
        jnp.bfloat16
    )
    squares_high = squares.astype(jnp.bfloat16)
    squares_low = (squares - squares_high.astype(jnp.float32)).astype(jnp.bfloat16)
    square_columns = jnp.zeros((row_count, 128), jnp.bfloat16)
    square_columns = square_columns.at[:, 0].set(squares_high).at[:, 1].set(squares_low)
    width = partials.shape[1]
    received_partials = lax.all_to_all(
        jnp.concatenate([partials, square_columns], axis=1), "tensor", 0, 0, tiled=True
    ).reshape(tensor_count, -1, width + 128)
    reduced = jnp.sum(received_partials[:, :, :width].astype(jnp.float32), axis=0)
    totals = jnp.sum(
        received_partials[:, :, width].astype(jnp.float32)
        + received_partials[:, :, width + 1].astype(jnp.float32),
        axis=0,
    )
    scale = lax.rsqrt(totals[:, None] / (local_inner * tensor_count) + 1e-05)
    mixed = (reduced * scale).astype(jnp.bfloat16)
    request_count = lengths.shape[0]
    request_ids = jnp.arange(request_count, dtype=jnp.int32)
    slot_request = jnp.sum(
        (slots[None, :] == request_ids[:, None]).astype(jnp.int32) * request_ids[None, :], axis=1
    )
    ends = jnp.take(starts + lengths - 1 - DRAFTS + accepted, slot_request)
    present = (ends >= first) & (ends < first + row_count)
    local_end = jnp.clip(ends - first, 0, row_count - 1)
    which = local_end // BLOCK
    place = local_end % BLOCK
    positions = jnp.arange(BLOCK, dtype=jnp.int32)
    bracket = jnp.zeros((request_count, local_heads, head_size, state_size), jnp.float32)
    coefficient = jnp.zeros((request_count, local_heads), jnp.float32)
    for block in range(block_count):
        in_block = (which == block) & present
        end_sums = jnp.take(decay_sum[block], place, axis=0)
        valid = (
            in_block[:, None]
            & (positions[None, :] <= place[:, None])
            & (segs[block][None, :] == slot_request[:, None])
        )
        weight = jnp.where(
            valid[..., None],
            jnp.exp(jnp.minimum(end_sums[:, None, :] - decay_sum[block][None], 0.0))
            * steps[block][None],
            0.0,
        )
        bracket = bracket + jnp.einsum(
            "rjhp,jn->rhpn",
            weight[..., None] * values[block][None],
            keys[block],
            preferred_element_type=jnp.float32,
        )
        carried = jnp.where(
            (in_block & (prior[block] == slot_request))[:, None], jnp.exp(end_sums), 0.0
        )
        bracket = bracket + carried[:, :, None, None] * zero_starts[block][None]
        coefficient = coefficient + carried * factors[block][None]
    outgoing = bracket + coefficient[:, :, None, None] * incoming[None]
    chunks = outgoing.astype(jnp.bfloat16).reshape(
        seq_count, request_count // seq_count, local_heads, head_size, state_size
    )
    pieces = [jnp.take(chunks, seq_index, axis=0).astype(jnp.float32)]
    for distance in range(1, seq_count):
        target = (seq_index + distance) % seq_count
        route = [(i, (i + distance) % seq_count) for i in range(seq_count)]
        pieces.append(
            lax.ppermute(jnp.take(chunks, target, axis=0), "seq", route).astype(jnp.float32)
        )
    mine = sum(pieces[1:], pieces[0])
    return (mixed, mine)


def solution(mesh):
    return jax.shard_map(
        per_device,
        mesh=mesh,
        in_specs=(
            P(("seq", "tensor"), None),
            P(None, "tensor"),
            P(None, "tensor"),
            P(None, "tensor"),
            P(),
            P(None, "tensor"),
            P("tensor"),
            P(),
            P(),
            P("tensor"),
            P("tensor"),
            P("tensor"),
            P("tensor"),
            P("tensor", None),
            P(),
            P(),
            P(),
        ),
        out_specs=(P(("seq", "tensor"), None), P("seq", "tensor", None, None)),
        check_vma=False,
    )
```

```python
import jax
import jax.numpy as jnp
from jax import lax
from jax.sharding import PartitionSpec as P

BLOCK = 256
DRAFTS = 16


HIGHEST_PRECISION = lax.Precision.HIGHEST


def passed_along(block, axis, distance):
    devices = range(lax.axis_size(axis))
    route = [(i - distance, i) for i in devices if i - distance in devices]
    return lax.ppermute(block, axis, route)


def segment_of(positions, starts):
    return jnp.sum((starts[None, :] <= positions[:, None]).astype(jnp.int32), axis=1) - 1


def per_device(
    tokens,
    in_gate,
    in_x,
    in_dt,
    in_bc,
    conv_x_weight,
    conv_x_bias,
    conv_bc_weight,
    conv_bc_bias,
    dt_bias,
    head_rate,
    skip_gain,
    norm_gain,
    out_weight,
    lengths,
    accepted,
    slots,
):
    local_inner = in_x.shape[1]
    local_heads = in_dt.shape[1]
    head_size = local_inner // local_heads
    state_size = in_bc.shape[1] // 2
    tensor_count = lax.axis_size("tensor")
    seq_count = lax.axis_size("seq")
    weight_all = jnp.concatenate([in_gate, in_x, in_dt, in_bc], axis=1)
    gathered = lax.all_to_all(
        jnp.tile(tokens, (lax.axis_size("tensor"), 1)), "tensor", 0, 0, tiled=True
    )
    projected = jnp.dot(
        gathered,
        weight_all,
        preferred_element_type=jnp.float32,
    )
    bc_inputs = projected[:, 2 * local_inner + local_heads :]
    gate = projected[:, :local_inner]
    raw_step = projected[:, 2 * local_inner : 2 * local_inner + local_heads]
    inputs = jnp.concatenate([projected[:, local_inner : 2 * local_inner], bc_inputs], axis=1)
    row_count = projected.shape[0]
    first = lax.axis_index("seq") * row_count
    starts = jnp.cumsum(lengths) - lengths
    segment = segment_of(first + jnp.arange(row_count, dtype=jnp.int32), starts)
    taps = conv_x_weight.shape[0]
    edge = passed_along(inputs[row_count - taps + 1 :], "seq", 1)
    edge_segment = segment_of(first - taps + 1 + jnp.arange(taps - 1, dtype=jnp.int32), starts)
    extended = jnp.concatenate([edge, inputs], axis=0)
    extended_segment = jnp.concatenate([edge_segment, segment])
    conv_weight = jnp.concatenate([conv_x_weight, conv_bc_weight], axis=1)
    conv_bias = jnp.concatenate([conv_x_bias, conv_bc_bias])
    conv = jnp.zeros_like(inputs) + conv_bias[None, :]
    for offset in range(taps):
        match = (extended_segment[offset : offset + row_count] == segment).astype(jnp.float32)
        conv = (
            conv
            + conv_weight[offset][None, :] * extended[offset : offset + row_count] * match[:, None]
        )
    active = jax.nn.silu(conv)
    block_count = row_count // BLOCK
    values = active[:, :local_inner].reshape(block_count, BLOCK, local_heads, head_size)
    keys = active[:, local_inner : local_inner + state_size].reshape(block_count, BLOCK, state_size)
    queries = active[:, local_inner + state_size :].reshape(block_count, BLOCK, state_size)
    step_size = jax.nn.softplus(raw_step + dt_bias[None, :])
    lower_ones = (
        jnp.arange(BLOCK)[:, None] >= jnp.arange(BLOCK)[None, :]
    ).astype(jnp.float32)
    decay_sum = jnp.einsum(
        "ij,cjh->cih",
        lower_ones,
        (-head_rate[None, :] * step_size).reshape(block_count, BLOCK, local_heads),
        precision=HIGHEST_PRECISION,
    )
    steps = step_size.reshape(block_count, BLOCK, local_heads)
    segs = segment.reshape(block_count, BLOCK)
    prior = segment_of(first + jnp.arange(block_count, dtype=jnp.int32) * BLOCK - 1, starts)
    lower = jnp.arange(BLOCK)[:, None] >= jnp.arange(BLOCK)[None, :]
    same = (segs[:, :, None] == segs[:, None, :]) & lower[None]
    spread = decay_sum[:, :, None, :] - decay_sum[:, None, :, :]
    decay = jnp.where(same[..., None], jnp.exp(jnp.minimum(spread, 0.0)), 0.0)
    gram = jnp.einsum("cin,cjn->cij", queries, keys, precision=HIGHEST_PRECISION)
    mixing = gram[..., None] * decay * steps[:, None, :, :]
    inner = jnp.einsum("cijh,cjhp->cihp", mixing, values, precision=HIGHEST_PRECISION)
    last_match = (segs == segs[:, -1:]).astype(jnp.float32)
    weight_last = jnp.exp(decay_sum[:, -1:, :] - decay_sum) * steps * last_match[..., None]
    local = jnp.einsum(
        "cjhp,cjn->chpn", weight_last[..., None] * values, keys, precision=HIGHEST_PRECISION
    )
    passes = jnp.exp(decay_sum[:, -1, :]) * (segs[:, -1] == prior).astype(jnp.float32)[:, None]

    empty = jnp.zeros((local_heads, head_size, state_size), jnp.float32)
    zero_start_list = []
    factor_list = []
    zero_end = empty
    factor_end = jnp.ones((local_heads,), jnp.float32)
    for block in range(block_count):
        zero_start_list.append(zero_end)
        factor_list.append(factor_end)
        zero_end = passes[block][:, None, None] * zero_end + local[block]
        factor_end = passes[block] * factor_end
    zero_starts = jnp.stack(zero_start_list)
    factors = jnp.stack(factor_list)

    factor_high = factor_end.astype(jnp.bfloat16)
    factor_low = (factor_end - factor_high.astype(jnp.float32)).astype(jnp.bfloat16)
    factor_rows = jnp.zeros((local_heads, 16, state_size), jnp.bfloat16)
    factor_rows = factor_rows.at[:, 0, :].set(factor_high[:, None])
    factor_rows = factor_rows.at[:, 1, :].set(factor_low[:, None])
    packed = jnp.concatenate([zero_end.astype(jnp.bfloat16), factor_rows], axis=1)
    sent = lax.all_to_all(jnp.tile(packed[None], (seq_count, 1, 1, 1)), "seq", 0, 0, tiled=True)
    sent_states = sent[:, :, :head_size]
    sent_factors = sent[:, :, head_size, 0].astype(jnp.float32) + sent[
        :, :, head_size + 1, 0
    ].astype(jnp.float32)
    seq_index = lax.axis_index("seq")
    incoming = empty
    for earlier in range(seq_count - 1):
        advanced = sent_factors[earlier][:, None, None] * incoming + sent_states[earlier].astype(
            jnp.float32
        )
        incoming = jnp.where(earlier < seq_index, advanced, incoming)
    block_states = zero_starts + factors[:, :, None, None] * incoming[None]
    keep = jnp.exp(decay_sum) * (segs == prior[:, None]).astype(jnp.float32)[..., None]
    outer = keep[..., None] * jnp.einsum(
        "cin,chpn->cihp", queries, block_states, precision=HIGHEST_PRECISION
    )
    output = (inner + outer + skip_gain[None, None, :, None] * values).reshape(
        row_count, local_inner
    )
    gated = output * jax.nn.silu(gate)
    squares = jnp.sum(gated * gated, axis=1)
    unscaled = (gated * norm_gain[None, :]).astype(jnp.bfloat16)
    partials = jnp.dot(unscaled, out_weight, preferred_element_type=jnp.float32).astype(
        jnp.bfloat16
    )
    squares_high = squares.astype(jnp.bfloat16)
    squares_low = (squares - squares_high.astype(jnp.float32)).astype(jnp.bfloat16)
    square_columns = jnp.zeros((row_count, 128), jnp.bfloat16)
    square_columns = square_columns.at[:, 0].set(squares_high).at[:, 1].set(squares_low)
    width = partials.shape[1]
    received_partials = lax.all_to_all(
        jnp.concatenate([partials, square_columns], axis=1), "tensor", 0, 0, tiled=True
    ).reshape(tensor_count, -1, width + 128)
    reduced = jnp.sum(received_partials[:, :, :width].astype(jnp.float32), axis=0)
    totals = jnp.sum(
        received_partials[:, :, width].astype(jnp.float32)
        + received_partials[:, :, width + 1].astype(jnp.float32),
        axis=0,
    )
    scale = lax.rsqrt(totals[:, None] / (local_inner * tensor_count) + 1e-05)
    mixed = (reduced * scale).astype(jnp.bfloat16)
    request_count = lengths.shape[0]
    request_ids = jnp.arange(request_count, dtype=jnp.int32)
    slot_request = jnp.sum(
        (slots[None, :] == request_ids[:, None]).astype(jnp.int32) * request_ids[None, :], axis=1
    )
    ends = jnp.take(starts + lengths - 1 - DRAFTS + accepted, slot_request)
    present = (ends >= first) & (ends < first + row_count)
    local_end = jnp.clip(ends - first, 0, row_count - 1)
    which = local_end // BLOCK
    place = local_end % BLOCK
    positions = jnp.arange(BLOCK, dtype=jnp.int32)
    bracket = jnp.zeros((request_count, local_heads, head_size, state_size), jnp.float32)
    coefficient = jnp.zeros((request_count, local_heads), jnp.float32)
    for block in range(block_count):
        in_block = (which == block) & present
        end_sums = jnp.take(decay_sum[block], place, axis=0)
        valid = (
            in_block[:, None]
            & (positions[None, :] <= place[:, None])
            & (segs[block][None, :] == slot_request[:, None])
        )
        weight = jnp.where(
            valid[..., None],
            jnp.exp(jnp.minimum(end_sums[:, None, :] - decay_sum[block][None], 0.0))
            * steps[block][None],
            0.0,
        )
        bracket = bracket + jnp.einsum(
            "rjhp,jn->rhpn",
            weight[..., None] * values[block][None],
            keys[block],
            preferred_element_type=jnp.float32,
        )
        carried = jnp.where(
            (in_block & (prior[block] == slot_request))[:, None], jnp.exp(end_sums), 0.0
        )
        bracket = bracket + carried[:, :, None, None] * zero_starts[block][None]
        coefficient = coefficient + carried * factors[block][None]
    outgoing = bracket + coefficient[:, :, None, None] * incoming[None]
    chunks = outgoing.astype(jnp.bfloat16).reshape(
        seq_count, request_count // seq_count, local_heads, head_size, state_size
    )
    pieces = [jnp.take(chunks, seq_index, axis=0).astype(jnp.float32)]
    for distance in range(1, seq_count):
        target = (seq_index + distance) % seq_count
        route = [(i, (i + distance) % seq_count) for i in range(seq_count)]
        pieces.append(
            lax.ppermute(jnp.take(chunks, target, axis=0), "seq", route).astype(jnp.float32)
        )
    mine = sum(pieces[1:], pieces[0])
    return (mixed, mine)


def solution(mesh):
    return jax.shard_map(
        per_device,
        mesh=mesh,
        in_specs=(
            P(("seq", "tensor"), None),
            P(None, "tensor"),
            P(None, "tensor"),
            P(None, "tensor"),
            P(),
            P(None, "tensor"),
            P("tensor"),
            P(),
            P(),
            P("tensor"),
            P("tensor"),
            P("tensor"),
            P("tensor"),
            P("tensor", None),
            P(),
            P(),
            P(),
        ),
        out_specs=(P(("seq", "tensor"), None), P("seq", "tensor", None, None)),
        check_vma=False,
    )
```

```python
import jax
import jax.numpy as jnp
from jax import lax
from jax.sharding import PartitionSpec as P

BLOCK = 256
DRAFTS = 16


HIGHEST_PRECISION = lax.Precision.HIGHEST


def passed_along(block, axis, distance):
    devices = range(lax.axis_size(axis))
    route = [(i - distance, i) for i in devices if i - distance in devices]
    return lax.ppermute(block, axis, route)


def segment_of(positions, starts):
    return jnp.sum((starts[None, :] <= positions[:, None]).astype(jnp.int32), axis=1) - 1


def per_device(
    tokens,
    in_gate,
    in_x,
    in_dt,
    in_bc,
    conv_x_weight,
    conv_x_bias,
    conv_bc_weight,
    conv_bc_bias,
    dt_bias,
    head_rate,
    skip_gain,
    norm_gain,
    out_weight,
    lengths,
    accepted,
    slots,
):
    local_inner = in_x.shape[1]
    local_heads = in_dt.shape[1]
    head_size = local_inner // local_heads
    state_size = in_bc.shape[1] // 2
    tensor_count = lax.axis_size("tensor")
    seq_count = lax.axis_size("seq")
    weight_all = jnp.concatenate([in_gate, in_x, in_dt, in_bc], axis=1)
    gathered = lax.all_to_all(
        jnp.tile(tokens, (lax.axis_size("tensor"), 1)), "tensor", 0, 0, tiled=True
    )
    projected = jnp.dot(
        gathered,
        weight_all,
        preferred_element_type=jnp.float32,
    )
    bc_inputs = projected[:, 2 * local_inner + local_heads :]
    gate = projected[:, :local_inner]
    raw_step = projected[:, 2 * local_inner : 2 * local_inner + local_heads]
    inputs = jnp.concatenate([projected[:, local_inner : 2 * local_inner], bc_inputs], axis=1)
    row_count = projected.shape[0]
    first = lax.axis_index("seq") * row_count
    starts = jnp.cumsum(lengths) - lengths
    segment = segment_of(first + jnp.arange(row_count, dtype=jnp.int32), starts)
    taps = conv_x_weight.shape[0]
    edge = passed_along(inputs[row_count - taps + 1 :], "seq", 1)
    edge_segment = segment_of(first - taps + 1 + jnp.arange(taps - 1, dtype=jnp.int32), starts)
    extended = jnp.concatenate([edge, inputs], axis=0)
    extended_segment = jnp.concatenate([edge_segment, segment])
    conv_weight = jnp.concatenate([conv_x_weight, conv_bc_weight], axis=1)
    conv_bias = jnp.concatenate([conv_x_bias, conv_bc_bias])
    conv = jnp.zeros_like(inputs) + conv_bias[None, :]
    for offset in range(taps):
        match = (extended_segment[offset : offset + row_count] == segment).astype(jnp.float32)
        conv = (
            conv
            + conv_weight[offset][None, :] * extended[offset : offset + row_count] * match[:, None]
        )
    active = jax.nn.silu(conv)
    block_count = row_count // BLOCK
    values = active[:, :local_inner].reshape(block_count, BLOCK, local_heads, head_size)
    keys = active[:, local_inner : local_inner + state_size].reshape(block_count, BLOCK, state_size)
    queries = active[:, local_inner + state_size :].reshape(block_count, BLOCK, state_size)
    step_size = jax.nn.softplus(raw_step + dt_bias[None, :])
    lower_ones = (
        jnp.arange(BLOCK)[:, None] >= jnp.arange(BLOCK)[None, :]
    ).astype(jnp.float32)
    decay_sum = jnp.einsum(
        "ij,cjh->cih",
        lower_ones,
        (-head_rate[None, :] * step_size).reshape(block_count, BLOCK, local_heads),
        precision=HIGHEST_PRECISION,
    )
    steps = step_size.reshape(block_count, BLOCK, local_heads)
    segs = segment.reshape(block_count, BLOCK)
    prior = segment_of(first + jnp.arange(block_count, dtype=jnp.int32) * BLOCK - 1, starts)
    lower = jnp.arange(BLOCK)[:, None] >= jnp.arange(BLOCK)[None, :]
    same = (segs[:, :, None] == segs[:, None, :]) & lower[None]
    spread = decay_sum[:, :, None, :] - decay_sum[:, None, :, :]
    decay = jnp.where(same[..., None], jnp.exp(jnp.minimum(spread, 0.0)), 0.0)
    gram = jnp.einsum("cin,cjn->cij", queries, keys, precision=HIGHEST_PRECISION)
    mixing = gram[..., None] * decay * steps[:, None, :, :]
    inner = jnp.einsum("cijh,cjhp->cihp", mixing, values, precision=HIGHEST_PRECISION)
    last_match = (segs == segs[:, -1:]).astype(jnp.float32)
    weight_last = jnp.exp(decay_sum[:, -1:, :] - decay_sum) * steps * last_match[..., None]
    local = jnp.einsum(
        "cjhp,cjn->chpn", weight_last[..., None] * values, keys, precision=HIGHEST_PRECISION
    )
    passes = jnp.exp(decay_sum[:, -1, :]) * (segs[:, -1] == prior).astype(jnp.float32)[:, None]

    empty = jnp.zeros((local_heads, head_size, state_size), jnp.float32)
    zero_start_list = []
    factor_list = []
    zero_end = empty
    factor_end = jnp.ones((local_heads,), jnp.float32)
    for block in range(block_count):
        zero_start_list.append(zero_end)
        factor_list.append(factor_end)
        zero_end = passes[block][:, None, None] * zero_end + local[block]
        factor_end = passes[block] * factor_end
    zero_starts = jnp.stack(zero_start_list)
    factors = jnp.stack(factor_list)

    factor_high = factor_end.astype(jnp.bfloat16)
    factor_low = (factor_end - factor_high.astype(jnp.float32)).astype(jnp.bfloat16)
    row_slot = jnp.arange(16)[None, :, None]
    factor_rows = jnp.where(
        row_slot == 0,
        factor_high[:, None, None],
        jnp.where(row_slot == 1, factor_low[:, None, None], jnp.zeros((), jnp.bfloat16)),
    )
    factor_rows = jnp.broadcast_to(factor_rows, (local_heads, 16, state_size))
    packed = jnp.concatenate([zero_end.astype(jnp.bfloat16), factor_rows], axis=1)
    sent = lax.all_to_all(jnp.tile(packed[None], (seq_count, 1, 1, 1)), "seq", 0, 0, tiled=True)
    sent_states = sent[:, :, :head_size]
    sent_factors = sent[:, :, head_size, 0].astype(jnp.float32) + sent[
        :, :, head_size + 1, 0
    ].astype(jnp.float32)
    seq_index = lax.axis_index("seq")
    incoming = empty
    for earlier in range(seq_count - 1):
        advanced = sent_factors[earlier][:, None, None] * incoming + sent_states[earlier].astype(
            jnp.float32
        )
        incoming = jnp.where(earlier < seq_index, advanced, incoming)
    block_states = zero_starts + factors[:, :, None, None] * incoming[None]
    keep = jnp.exp(decay_sum) * (segs == prior[:, None]).astype(jnp.float32)[..., None]
    outer = keep[..., None] * jnp.einsum(
        "cin,chpn->cihp", queries, block_states, precision=HIGHEST_PRECISION
    )
    output = (inner + outer + skip_gain[None, None, :, None] * values).reshape(
        row_count, local_inner
    )
    gated = output * jax.nn.silu(gate)
    squares = jnp.sum(gated * gated, axis=1)
    unscaled = (gated * norm_gain[None, :]).astype(jnp.bfloat16)
    partials = jnp.dot(unscaled, out_weight, preferred_element_type=jnp.float32).astype(
        jnp.bfloat16
    )
    squares_high = squares.astype(jnp.bfloat16)
    squares_low = (squares - squares_high.astype(jnp.float32)).astype(jnp.bfloat16)
    column_slot = jnp.arange(128)[None, :]
    square_columns = jnp.where(
        column_slot == 0,
        squares_high[:, None],
        jnp.where(column_slot == 1, squares_low[:, None], jnp.zeros((), jnp.bfloat16)),
    )
    width = partials.shape[1]
    received_partials = lax.all_to_all(
        jnp.concatenate([partials, square_columns], axis=1), "tensor", 0, 0, tiled=True
    ).reshape(tensor_count, -1, width + 128)
    reduced = jnp.sum(received_partials[:, :, :width].astype(jnp.float32), axis=0)
    totals = jnp.sum(
        received_partials[:, :, width].astype(jnp.float32)
        + received_partials[:, :, width + 1].astype(jnp.float32),
        axis=0,
    )
    scale = lax.rsqrt(totals[:, None] / (local_inner * tensor_count) + 1e-05)
    mixed = (reduced * scale).astype(jnp.bfloat16)
    request_count = lengths.shape[0]
    request_ids = jnp.arange(request_count, dtype=jnp.int32)
    slot_request = jnp.sum(
        (slots[None, :] == request_ids[:, None]).astype(jnp.int32) * request_ids[None, :], axis=1
    )
    ends = jnp.take(starts + lengths - 1 - DRAFTS + accepted, slot_request)
    present = (ends >= first) & (ends < first + row_count)
    local_end = jnp.clip(ends - first, 0, row_count - 1)
    which = local_end // BLOCK
    place = local_end % BLOCK
    positions = jnp.arange(BLOCK, dtype=jnp.int32)
    bracket = jnp.zeros((request_count, local_heads, head_size, state_size), jnp.float32)
    coefficient = jnp.zeros((request_count, local_heads), jnp.float32)
    for block in range(block_count):
        in_block = (which == block) & present
        end_sums = jnp.take(decay_sum[block], place, axis=0)
        valid = (
            in_block[:, None]
            & (positions[None, :] <= place[:, None])
            & (segs[block][None, :] == slot_request[:, None])
        )
        weight = jnp.where(
            valid[..., None],
            jnp.exp(jnp.minimum(end_sums[:, None, :] - decay_sum[block][None], 0.0))
            * steps[block][None],
            0.0,
        )
        bracket = bracket + jnp.einsum(
            "rjhp,jn->rhpn",
            weight[..., None] * values[block][None],
            keys[block],
            preferred_element_type=jnp.float32,
        )
        carried = jnp.where(
            (in_block & (prior[block] == slot_request))[:, None], jnp.exp(end_sums), 0.0
        )
        bracket = bracket + carried[:, :, None, None] * zero_starts[block][None]
        coefficient = coefficient + carried * factors[block][None]
    outgoing = bracket + coefficient[:, :, None, None] * incoming[None]
    chunks = outgoing.astype(jnp.bfloat16).reshape(
        seq_count, request_count // seq_count, local_heads, head_size, state_size
    )
    pieces = [jnp.take(chunks, seq_index, axis=0).astype(jnp.float32)]
    for distance in range(1, seq_count):
        target = (seq_index + distance) % seq_count
        route = [(i, (i + distance) % seq_count) for i in range(seq_count)]
        pieces.append(
            lax.ppermute(jnp.take(chunks, target, axis=0), "seq", route).astype(jnp.float32)
        )
    mine = sum(pieces[1:], pieces[0])
    return (mixed, mine)


def solution(mesh):
    return jax.shard_map(
        per_device,
        mesh=mesh,
        in_specs=(
            P(("seq", "tensor"), None),
            P(None, "tensor"),
            P(None, "tensor"),
            P(None, "tensor"),
            P(),
            P(None, "tensor"),
            P("tensor"),
            P(),
            P(),
            P("tensor"),
            P("tensor"),
            P("tensor"),
            P("tensor"),
            P("tensor", None),
            P(),
            P(),
            P(),
        ),
        out_specs=(P(("seq", "tensor"), None), P("seq", "tensor", None, None)),
        check_vma=False,
    )
```

```python
import jax
import jax.numpy as jnp
from jax import lax
from jax.sharding import PartitionSpec as P

BLOCK = 256
DRAFTS = 16


HIGHEST_PRECISION = lax.Precision.HIGHEST
HIGH_PRECISION = lax.Precision.HIGH


def passed_along(block, axis, distance):
    devices = range(lax.axis_size(axis))
    route = [(i - distance, i) for i in devices if i - distance in devices]
    return lax.ppermute(block, axis, route)


def segment_of(positions, starts):
    return jnp.sum((starts[None, :] <= positions[:, None]).astype(jnp.int32), axis=1) - 1


def per_device(
    tokens,
    in_gate,
    in_x,
    in_dt,
    in_bc,
    conv_x_weight,
    conv_x_bias,
    conv_bc_weight,
    conv_bc_bias,
    dt_bias,
    head_rate,
    skip_gain,
    norm_gain,
    out_weight,
    lengths,
    accepted,
    slots,
):
    local_inner = in_x.shape[1]
    local_heads = in_dt.shape[1]
    head_size = local_inner // local_heads
    state_size = in_bc.shape[1] // 2
    tensor_count = lax.axis_size("tensor")
    seq_count = lax.axis_size("seq")
    weight_all = jnp.concatenate([in_gate, in_x, in_dt, in_bc], axis=1)
    gathered = lax.all_to_all(
        jnp.tile(tokens, (lax.axis_size("tensor"), 1)), "tensor", 0, 0, tiled=True
    )
    projected = jnp.dot(
        gathered,
        weight_all,
        preferred_element_type=jnp.float32,
    )
    bc_inputs = projected[:, 2 * local_inner + local_heads :]
    gate = projected[:, :local_inner]
    raw_step = projected[:, 2 * local_inner : 2 * local_inner + local_heads]
    inputs = jnp.concatenate([projected[:, local_inner : 2 * local_inner], bc_inputs], axis=1)
    row_count = projected.shape[0]
    first = lax.axis_index("seq") * row_count
    starts = jnp.cumsum(lengths) - lengths
    segment = segment_of(first + jnp.arange(row_count, dtype=jnp.int32), starts)
    taps = conv_x_weight.shape[0]
    edge = passed_along(inputs[row_count - taps + 1 :], "seq", 1)
    edge_segment = segment_of(first - taps + 1 + jnp.arange(taps - 1, dtype=jnp.int32), starts)
    extended = jnp.concatenate([edge, inputs], axis=0)
    extended_segment = jnp.concatenate([edge_segment, segment])
    conv_weight = jnp.concatenate([conv_x_weight, conv_bc_weight], axis=1)
    conv_bias = jnp.concatenate([conv_x_bias, conv_bc_bias])
    conv = jnp.zeros_like(inputs) + conv_bias[None, :]
    for offset in range(taps):
        match = (extended_segment[offset : offset + row_count] == segment).astype(jnp.float32)
        conv = (
            conv
            + conv_weight[offset][None, :] * extended[offset : offset + row_count] * match[:, None]
        )
    active = jax.nn.silu(conv)
    block_count = row_count // BLOCK
    values = active[:, :local_inner].reshape(block_count, BLOCK, local_heads, head_size)
    keys = active[:, local_inner : local_inner + state_size].reshape(block_count, BLOCK, state_size)
    queries = active[:, local_inner + state_size :].reshape(block_count, BLOCK, state_size)
    step_size = jax.nn.softplus(raw_step + dt_bias[None, :])
    lower_ones = (
        jnp.arange(BLOCK)[:, None] >= jnp.arange(BLOCK)[None, :]
    ).astype(jnp.float32)
    decay_sum = jnp.einsum(
        "ij,cjh->cih",
        lower_ones,
        (-head_rate[None, :] * step_size).reshape(block_count, BLOCK, local_heads),
        precision=HIGHEST_PRECISION,
    )
    steps = step_size.reshape(block_count, BLOCK, local_heads)
    segs = segment.reshape(block_count, BLOCK)
    prior = segment_of(first + jnp.arange(block_count, dtype=jnp.int32) * BLOCK - 1, starts)
    lower = jnp.arange(BLOCK)[:, None] >= jnp.arange(BLOCK)[None, :]
    same = (segs[:, :, None] == segs[:, None, :]) & lower[None]
    spread = decay_sum[:, :, None, :] - decay_sum[:, None, :, :]
    decay = jnp.where(same[..., None], jnp.exp(jnp.minimum(spread, 0.0)), 0.0)
    gram = jnp.einsum("cin,cjn->cij", queries, keys, precision=HIGH_PRECISION)
    mixing = gram[..., None] * decay * steps[:, None, :, :]
    inner = jnp.einsum("cijh,cjhp->cihp", mixing, values, precision=HIGH_PRECISION)
    last_match = (segs == segs[:, -1:]).astype(jnp.float32)
    weight_last = jnp.exp(decay_sum[:, -1:, :] - decay_sum) * steps * last_match[..., None]
    local = jnp.einsum(
        "cjhp,cjn->chpn", weight_last[..., None] * values, keys, precision=HIGH_PRECISION
    )
    passes = jnp.exp(decay_sum[:, -1, :]) * (segs[:, -1] == prior).astype(jnp.float32)[:, None]

    empty = jnp.zeros((local_heads, head_size, state_size), jnp.float32)
    zero_start_list = []
    factor_list = []
    zero_end = empty
    factor_end = jnp.ones((local_heads,), jnp.float32)
    for block in range(block_count):
        zero_start_list.append(zero_end)
        factor_list.append(factor_end)
        zero_end = passes[block][:, None, None] * zero_end + local[block]
        factor_end = passes[block] * factor_end
    zero_starts = jnp.stack(zero_start_list)
    factors = jnp.stack(factor_list)

    factor_high = factor_end.astype(jnp.bfloat16)
    factor_low = (factor_end - factor_high.astype(jnp.float32)).astype(jnp.bfloat16)
    row_slot = jnp.arange(16)[None, :, None]
    factor_rows = jnp.where(
        row_slot == 0,
        factor_high[:, None, None],
        jnp.where(row_slot == 1, factor_low[:, None, None], jnp.zeros((), jnp.bfloat16)),
    )
    factor_rows = jnp.broadcast_to(factor_rows, (local_heads, 16, state_size))
    packed = jnp.concatenate([zero_end.astype(jnp.bfloat16), factor_rows], axis=1)
    sent = lax.all_to_all(jnp.tile(packed[None], (seq_count, 1, 1, 1)), "seq", 0, 0, tiled=True)
    sent_states = sent[:, :, :head_size]
    sent_factors = sent[:, :, head_size, 0].astype(jnp.float32) + sent[
        :, :, head_size + 1, 0
    ].astype(jnp.float32)
    seq_index = lax.axis_index("seq")
    incoming = empty
    for earlier in range(seq_count - 1):
        advanced = sent_factors[earlier][:, None, None] * incoming + sent_states[earlier].astype(
            jnp.float32
        )
        incoming = jnp.where(earlier < seq_index, advanced, incoming)
    block_states = zero_starts + factors[:, :, None, None] * incoming[None]
    keep = jnp.exp(decay_sum) * (segs == prior[:, None]).astype(jnp.float32)[..., None]
    outer = keep[..., None] * jnp.einsum(
        "cin,chpn->cihp", queries, block_states, precision=HIGH_PRECISION
    )
    output = (inner + outer + skip_gain[None, None, :, None] * values).reshape(
        row_count, local_inner
    )
    gated = output * jax.nn.silu(gate)
    squares = jnp.sum(gated * gated, axis=1)
    unscaled = (gated * norm_gain[None, :]).astype(jnp.bfloat16)
    partials = jnp.dot(unscaled, out_weight, preferred_element_type=jnp.float32).astype(
        jnp.bfloat16
    )
    squares_high = squares.astype(jnp.bfloat16)
    squares_low = (squares - squares_high.astype(jnp.float32)).astype(jnp.bfloat16)
    column_slot = jnp.arange(128)[None, :]
    square_columns = jnp.where(
        column_slot == 0,
        squares_high[:, None],
        jnp.where(column_slot == 1, squares_low[:, None], jnp.zeros((), jnp.bfloat16)),
    )
    width = partials.shape[1]
    received_partials = lax.all_to_all(
        jnp.concatenate([partials, square_columns], axis=1), "tensor", 0, 0, tiled=True
    ).reshape(tensor_count, -1, width + 128)
    totals = jnp.sum(
        received_partials[:, :, width].astype(jnp.float32)
        + received_partials[:, :, width + 1].astype(jnp.float32),
        axis=0,
    )
    scale = lax.rsqrt(totals[:, None] / (local_inner * tensor_count) + 1e-05)
    mixed = jnp.sum(
        received_partials[:, :, :width].astype(jnp.float32) * scale[None], axis=0
    ).astype(jnp.bfloat16)
    request_count = lengths.shape[0]
    request_ids = jnp.arange(request_count, dtype=jnp.int32)
    slot_request = jnp.sum(
        (slots[None, :] == request_ids[:, None]).astype(jnp.int32) * request_ids[None, :], axis=1
    )
    ends = jnp.take(starts + lengths - 1 - DRAFTS + accepted, slot_request)
    present = (ends >= first) & (ends < first + row_count)
    local_end = jnp.clip(ends - first, 0, row_count - 1)
    which = local_end // BLOCK
    place = local_end % BLOCK
    positions = jnp.arange(BLOCK, dtype=jnp.int32)
    bracket = jnp.zeros((request_count, local_heads, head_size, state_size), jnp.float32)
    coefficient = jnp.zeros((request_count, local_heads), jnp.float32)
    for block in range(block_count):
        in_block = (which == block) & present
        end_sums = jnp.take(decay_sum[block], place, axis=0)
        valid = (
            in_block[:, None]
            & (positions[None, :] <= place[:, None])
            & (segs[block][None, :] == slot_request[:, None])
        )
        weight = jnp.where(
            valid[..., None],
            jnp.exp(jnp.minimum(end_sums[:, None, :] - decay_sum[block][None], 0.0))
            * steps[block][None],
            0.0,
        )
        bracket = bracket + jnp.einsum(
            "rjhp,jn->rhpn",
            weight[..., None] * values[block][None],
            keys[block],
            preferred_element_type=jnp.float32,
        )
        carried = jnp.where(
            (in_block & (prior[block] == slot_request))[:, None], jnp.exp(end_sums), 0.0
        )
        bracket = bracket + carried[:, :, None, None] * zero_starts[block][None]
        coefficient = coefficient + carried * factors[block][None]
    outgoing = bracket + coefficient[:, :, None, None] * incoming[None]
    chunks = outgoing.astype(jnp.bfloat16).reshape(
        seq_count, request_count // seq_count, local_heads, head_size, state_size
    )
    pieces = [jnp.take(chunks, seq_index, axis=0).astype(jnp.float32)]
    for distance in range(1, seq_count):
        target = (seq_index + distance) % seq_count
        route = [(i, (i + distance) % seq_count) for i in range(seq_count)]
        pieces.append(
            lax.ppermute(jnp.take(chunks, target, axis=0), "seq", route).astype(jnp.float32)
        )
    mine = sum(pieces[1:], pieces[0])
    return (mixed, mine)


def solution(mesh):
    return jax.shard_map(
        per_device,
        mesh=mesh,
        in_specs=(
            P(("seq", "tensor"), None),
            P(None, "tensor"),
            P(None, "tensor"),
            P(None, "tensor"),
            P(),
            P(None, "tensor"),
            P("tensor"),
            P(),
            P(),
            P("tensor"),
            P("tensor"),
            P("tensor"),
            P("tensor"),
            P("tensor", None),
            P(),
            P(),
            P(),
        ),
        out_specs=(P(("seq", "tensor"), None), P("seq", "tensor", None, None)),
        check_vma=False,
    )
```

```python
import jax
import jax.numpy as jnp
from jax import lax
from jax.sharding import PartitionSpec as P

BLOCK = 256
DRAFTS = 16


HIGHEST_PRECISION = lax.Precision.HIGHEST
HIGH_PRECISION = lax.Precision.HIGH


def passed_along(block, axis, distance):
    devices = range(lax.axis_size(axis))
    route = [(i - distance, i) for i in devices if i - distance in devices]
    return lax.ppermute(block, axis, route)


def segment_of(positions, starts):
    return jnp.sum((starts[None, :] <= positions[:, None]).astype(jnp.int32), axis=1) - 1


def per_device(
    tokens,
    in_gate,
    in_x,
    in_dt,
    in_bc,
    conv_x_weight,
    conv_x_bias,
    conv_bc_weight,
    conv_bc_bias,
    dt_bias,
    head_rate,
    skip_gain,
    norm_gain,
    out_weight,
    lengths,
    accepted,
    slots,
):
    local_inner = in_x.shape[1]
    local_heads = in_dt.shape[1]
    head_size = local_inner // local_heads
    state_size = in_bc.shape[1] // 2
    tensor_count = lax.axis_size("tensor")
    seq_count = lax.axis_size("seq")
    gathered = lax.all_to_all(
        jnp.tile(tokens, (lax.axis_size("tensor"), 1)), "tensor", 0, 0, tiled=True
    )
    weight_state = jnp.concatenate([in_x, in_dt, in_bc[:, :state_size]], axis=1)
    weight_read = jnp.concatenate([in_gate, in_bc[:, state_size:]], axis=1)
    projected_state = jnp.dot(gathered, weight_state, preferred_element_type=jnp.float32)
    raw_step = projected_state[:, local_inner : local_inner + local_heads]
    state_inputs = jnp.concatenate(
        [projected_state[:, :local_inner], projected_state[:, local_inner + local_heads :]], axis=1
    )
    row_count = gathered.shape[0]
    first = lax.axis_index("seq") * row_count
    starts = jnp.cumsum(lengths) - lengths
    segment = segment_of(first + jnp.arange(row_count, dtype=jnp.int32), starts)
    taps = conv_x_weight.shape[0]
    edge_segment = segment_of(first - taps + 1 + jnp.arange(taps - 1, dtype=jnp.int32), starts)
    extended_segment = jnp.concatenate([edge_segment, segment])

    def convolved(inputs, conv_weight, conv_bias):
        edge = passed_along(inputs[row_count - taps + 1 :], "seq", 1)
        extended = jnp.concatenate([edge, inputs], axis=0)
        conv = jnp.zeros_like(inputs) + conv_bias[None, :]
        for offset in range(taps):
            match = (extended_segment[offset : offset + row_count] == segment).astype(jnp.float32)
            conv = (
                conv
                + conv_weight[offset][None, :]
                * extended[offset : offset + row_count]
                * match[:, None]
            )
        return jax.nn.silu(conv)

    active = convolved(
        state_inputs,
        jnp.concatenate([conv_x_weight, conv_bc_weight[:, :state_size]], axis=1),
        jnp.concatenate([conv_x_bias, conv_bc_bias[:state_size]]),
    )
    block_count = row_count // BLOCK
    values = active[:, :local_inner].reshape(block_count, BLOCK, local_heads, head_size)
    keys = active[:, local_inner:].reshape(block_count, BLOCK, state_size)
    step_size = jax.nn.softplus(raw_step + dt_bias[None, :])
    lower_ones = (
        jnp.arange(BLOCK)[:, None] >= jnp.arange(BLOCK)[None, :]
    ).astype(jnp.float32)
    decay_sum = jnp.einsum(
        "ij,cjh->cih",
        lower_ones,
        (-head_rate[None, :] * step_size).reshape(block_count, BLOCK, local_heads),
        precision=HIGHEST_PRECISION,
    )
    steps = step_size.reshape(block_count, BLOCK, local_heads)
    segs = segment.reshape(block_count, BLOCK)
    prior = segment_of(first + jnp.arange(block_count, dtype=jnp.int32) * BLOCK - 1, starts)
    lower = jnp.arange(BLOCK)[:, None] >= jnp.arange(BLOCK)[None, :]
    same = (segs[:, :, None] == segs[:, None, :]) & lower[None]
    spread = decay_sum[:, :, None, :] - decay_sum[:, None, :, :]
    decay = jnp.where(same[..., None], jnp.exp(jnp.minimum(spread, 0.0)), 0.0)
    last_match = (segs == segs[:, -1:]).astype(jnp.float32)
    weight_last = jnp.exp(decay_sum[:, -1:, :] - decay_sum) * steps * last_match[..., None]
    local = jnp.einsum(
        "cjhp,cjn->chpn", weight_last[..., None] * values, keys, precision=HIGH_PRECISION
    )
    passes = jnp.exp(decay_sum[:, -1, :]) * (segs[:, -1] == prior).astype(jnp.float32)[:, None]

    empty = jnp.zeros((local_heads, head_size, state_size), jnp.float32)
    zero_start_list = []
    factor_list = []
    zero_end = empty
    factor_end = jnp.ones((local_heads,), jnp.float32)
    for block in range(block_count):
        zero_start_list.append(zero_end)
        factor_list.append(factor_end)
        zero_end = passes[block][:, None, None] * zero_end + local[block]
        factor_end = passes[block] * factor_end
    zero_starts = jnp.stack(zero_start_list)
    factors = jnp.stack(factor_list)

    factor_high = factor_end.astype(jnp.bfloat16)
    factor_low = (factor_end - factor_high.astype(jnp.float32)).astype(jnp.bfloat16)
    row_slot = jnp.arange(16)[None, :, None]
    factor_rows = jnp.where(
        row_slot == 0,
        factor_high[:, None, None],
        jnp.where(row_slot == 1, factor_low[:, None, None], jnp.zeros((), jnp.bfloat16)),
    )
    factor_rows = jnp.broadcast_to(factor_rows, (local_heads, 16, state_size))
    packed = jnp.concatenate([zero_end.astype(jnp.bfloat16), factor_rows], axis=1)
    relay_message, gathered_late = lax.optimization_barrier(
        (jnp.tile(packed[None], (seq_count, 1, 1, 1)), gathered)
    )
    sent = lax.all_to_all(relay_message, "seq", 0, 0, tiled=True)
    projected_read = jnp.dot(gathered_late, weight_read, preferred_element_type=jnp.float32)
    gate = projected_read[:, :local_inner]
    read_inputs = projected_read[:, local_inner:]
    read_active = convolved(read_inputs, conv_bc_weight[:, state_size:], conv_bc_bias[state_size:])
    queries = read_active.reshape(block_count, BLOCK, state_size)
    gram = jnp.einsum("cin,cjn->cij", queries, keys, precision=HIGH_PRECISION)
    mixing = gram[..., None] * decay * steps[:, None, :, :]
    inner = jnp.einsum("cijh,cjhp->cihp", mixing, values, precision=HIGH_PRECISION)
    sent_states = sent[:, :, :head_size]
    sent_factors = sent[:, :, head_size, 0].astype(jnp.float32) + sent[
        :, :, head_size + 1, 0
    ].astype(jnp.float32)
    seq_index = lax.axis_index("seq")
    incoming = empty
    for earlier in range(seq_count - 1):
        advanced = sent_factors[earlier][:, None, None] * incoming + sent_states[earlier].astype(
            jnp.float32
        )
        incoming = jnp.where(earlier < seq_index, advanced, incoming)
    block_states = zero_starts + factors[:, :, None, None] * incoming[None]
    keep = jnp.exp(decay_sum) * (segs == prior[:, None]).astype(jnp.float32)[..., None]
    outer = keep[..., None] * jnp.einsum(
        "cin,chpn->cihp", queries, block_states, precision=HIGH_PRECISION
    )
    output = (inner + outer + skip_gain[None, None, :, None] * values).reshape(
        row_count, local_inner
    )
    gated = output * jax.nn.silu(gate)
    squares = jnp.sum(gated * gated, axis=1)
    unscaled = (gated * norm_gain[None, :]).astype(jnp.bfloat16)
    partials = jnp.dot(unscaled, out_weight, preferred_element_type=jnp.float32).astype(
        jnp.bfloat16
    )
    squares_high = squares.astype(jnp.bfloat16)
    squares_low = (squares - squares_high.astype(jnp.float32)).astype(jnp.bfloat16)
    column_slot = jnp.arange(128)[None, :]
    square_columns = jnp.where(
        column_slot == 0,
        squares_high[:, None],
        jnp.where(column_slot == 1, squares_low[:, None], jnp.zeros((), jnp.bfloat16)),
    )
    width = partials.shape[1]
    received_partials = lax.all_to_all(
        jnp.concatenate([partials, square_columns], axis=1), "tensor", 0, 0, tiled=True
    ).reshape(tensor_count, -1, width + 128)
    totals = jnp.sum(
        received_partials[:, :, width].astype(jnp.float32)
        + received_partials[:, :, width + 1].astype(jnp.float32),
        axis=0,
    )
    scale = lax.rsqrt(totals[:, None] / (local_inner * tensor_count) + 1e-05)
    mixed = jnp.sum(
        received_partials[:, :, :width].astype(jnp.float32) * scale[None], axis=0
    ).astype(jnp.bfloat16)
    request_count = lengths.shape[0]
    request_ids = jnp.arange(request_count, dtype=jnp.int32)
    slot_request = jnp.sum(
        (slots[None, :] == request_ids[:, None]).astype(jnp.int32) * request_ids[None, :], axis=1
    )
    ends = jnp.take(starts + lengths - 1 - DRAFTS + accepted, slot_request)
    present = (ends >= first) & (ends < first + row_count)
    local_end = jnp.clip(ends - first, 0, row_count - 1)
    which = local_end // BLOCK
    place = local_end % BLOCK
    positions = jnp.arange(BLOCK, dtype=jnp.int32)
    bracket = jnp.zeros((request_count, local_heads, head_size, state_size), jnp.float32)
    coefficient = jnp.zeros((request_count, local_heads), jnp.float32)
    for block in range(block_count):
        in_block = (which == block) & present
        end_sums = jnp.take(decay_sum[block], place, axis=0)
        valid = (
            in_block[:, None]
            & (positions[None, :] <= place[:, None])
            & (segs[block][None, :] == slot_request[:, None])
        )
        weight = jnp.where(
            valid[..., None],
            jnp.exp(jnp.minimum(end_sums[:, None, :] - decay_sum[block][None], 0.0))
            * steps[block][None],
            0.0,
        )
        bracket = bracket + jnp.einsum(
            "rjhp,jn->rhpn",
            weight[..., None] * values[block][None],
            keys[block],
            preferred_element_type=jnp.float32,
        )
        carried = jnp.where(
            (in_block & (prior[block] == slot_request))[:, None], jnp.exp(end_sums), 0.0
        )
        bracket = bracket + carried[:, :, None, None] * zero_starts[block][None]
        coefficient = coefficient + carried * factors[block][None]
    outgoing = bracket + coefficient[:, :, None, None] * incoming[None]
    chunks = outgoing.astype(jnp.bfloat16).reshape(
        seq_count, request_count // seq_count, local_heads, head_size, state_size
    )
    pieces = [jnp.take(chunks, seq_index, axis=0).astype(jnp.float32)]
    for distance in range(1, seq_count):
        target = (seq_index + distance) % seq_count
        route = [(i, (i + distance) % seq_count) for i in range(seq_count)]
        pieces.append(
            lax.ppermute(jnp.take(chunks, target, axis=0), "seq", route).astype(jnp.float32)
        )
    mine = sum(pieces[1:], pieces[0])
    return (mixed, mine)


def solution(mesh):
    return jax.shard_map(
        per_device,
        mesh=mesh,
        in_specs=(
            P(("seq", "tensor"), None),
            P(None, "tensor"),
            P(None, "tensor"),
            P(None, "tensor"),
            P(),
            P(None, "tensor"),
            P("tensor"),
            P(),
            P(),
            P("tensor"),
            P("tensor"),
            P("tensor"),
            P("tensor"),
            P("tensor", None),
            P(),
            P(),
            P(),
        ),
        out_specs=(P(("seq", "tensor"), None), P("seq", "tensor", None, None)),
        check_vma=False,
    )
```

```python
import jax
import jax.numpy as jnp
from jax import lax
from jax.sharding import PartitionSpec as P

BLOCK = 256
DRAFTS = 16


HIGHEST_PRECISION = lax.Precision.HIGHEST
HIGH_PRECISION = lax.Precision.HIGH


def passed_along(block, axis, distance):
    devices = range(lax.axis_size(axis))
    route = [(i - distance, i) for i in devices if i - distance in devices]
    return lax.ppermute(block, axis, route)


def segment_of(positions, starts):
    return jnp.sum((starts[None, :] <= positions[:, None]).astype(jnp.int32), axis=1) - 1


def per_device(
    tokens,
    in_gate,
    in_x,
    in_dt,
    in_bc,
    conv_x_weight,
    conv_x_bias,
    conv_bc_weight,
    conv_bc_bias,
    dt_bias,
    head_rate,
    skip_gain,
    norm_gain,
    out_weight,
    lengths,
    accepted,
    slots,
):
    local_inner = in_x.shape[1]
    local_heads = in_dt.shape[1]
    head_size = local_inner // local_heads
    state_size = in_bc.shape[1] // 2
    tensor_count = lax.axis_size("tensor")
    seq_count = lax.axis_size("seq")
    weight_all = jnp.concatenate([in_gate, in_x, in_dt, in_bc], axis=1)
    gathered = lax.all_to_all(
        jnp.tile(tokens, (lax.axis_size("tensor"), 1)), "tensor", 0, 0, tiled=True
    )
    projected = jnp.dot(
        gathered,
        weight_all,
        preferred_element_type=jnp.float32,
    )
    bc_inputs = projected[:, 2 * local_inner + local_heads :]
    gate = projected[:, :local_inner]
    raw_step = projected[:, 2 * local_inner : 2 * local_inner + local_heads]
    inputs = jnp.concatenate([projected[:, local_inner : 2 * local_inner], bc_inputs], axis=1)
    row_count = projected.shape[0]
    first = lax.axis_index("seq") * row_count
    starts = jnp.cumsum(lengths) - lengths
    segment = segment_of(first + jnp.arange(row_count, dtype=jnp.int32), starts)
    taps = conv_x_weight.shape[0]
    edge = passed_along(inputs[row_count - taps + 1 :], "seq", 1)
    edge_segment = segment_of(first - taps + 1 + jnp.arange(taps - 1, dtype=jnp.int32), starts)
    extended = jnp.concatenate([edge, inputs], axis=0)
    extended_segment = jnp.concatenate([edge_segment, segment])
    conv_weight = jnp.concatenate([conv_x_weight, conv_bc_weight], axis=1)
    conv_bias = jnp.concatenate([conv_x_bias, conv_bc_bias])
    conv = jnp.zeros_like(inputs) + conv_bias[None, :]
    for offset in range(taps):
        match = (extended_segment[offset : offset + row_count] == segment).astype(jnp.float32)
        conv = (
            conv
            + conv_weight[offset][None, :] * extended[offset : offset + row_count] * match[:, None]
        )
    active = jax.nn.silu(conv)
    block_count = row_count // BLOCK
    values = active[:, :local_inner].reshape(block_count, BLOCK, local_heads, head_size)
    keys = active[:, local_inner : local_inner + state_size].reshape(block_count, BLOCK, state_size)
    queries = active[:, local_inner + state_size :].reshape(block_count, BLOCK, state_size)
    step_size = jax.nn.softplus(raw_step + dt_bias[None, :])
    lower_ones = (
        jnp.arange(BLOCK)[:, None] >= jnp.arange(BLOCK)[None, :]
    ).astype(jnp.float32)
    decay_sum = jnp.einsum(
        "ij,cjh->cih",
        lower_ones,
        (-head_rate[None, :] * step_size).reshape(block_count, BLOCK, local_heads),
        precision=HIGHEST_PRECISION,
    )
    steps = step_size.reshape(block_count, BLOCK, local_heads)
    segs = segment.reshape(block_count, BLOCK)
    prior = segment_of(first + jnp.arange(block_count, dtype=jnp.int32) * BLOCK - 1, starts)
    lower = jnp.arange(BLOCK)[:, None] >= jnp.arange(BLOCK)[None, :]
    same = (segs[:, :, None] == segs[:, None, :]) & lower[None]
    spread = decay_sum[:, :, None, :] - decay_sum[:, None, :, :]
    decay = jnp.where(same[..., None], jnp.exp(jnp.minimum(spread, 0.0)), 0.0)
    gram = jnp.einsum("cin,cjn->cij", queries, keys, precision=HIGH_PRECISION)
    mixing = gram[..., None] * decay * steps[:, None, :, :]
    inner = jnp.einsum("cijh,cjhp->cihp", mixing, values, precision=HIGH_PRECISION)
    last_match = (segs == segs[:, -1:]).astype(jnp.float32)
    weight_last = jnp.exp(decay_sum[:, -1:, :] - decay_sum) * steps * last_match[..., None]
    local = jnp.einsum(
        "cjhp,cjn->chpn", weight_last[..., None] * values, keys, precision=HIGH_PRECISION
    )
    passes = jnp.exp(decay_sum[:, -1, :]) * (segs[:, -1] == prior).astype(jnp.float32)[:, None]

    empty = jnp.zeros((local_heads, head_size, state_size), jnp.float32)
    zero_start_list = []
    factor_list = []
    zero_end = empty
    factor_end = jnp.ones((local_heads,), jnp.float32)
    for block in range(block_count):
        zero_start_list.append(zero_end)
        factor_list.append(factor_end)
        zero_end = passes[block][:, None, None] * zero_end + local[block]
        factor_end = passes[block] * factor_end
    zero_starts = jnp.stack(zero_start_list)
    factors = jnp.stack(factor_list)

    factor_high = factor_end.astype(jnp.bfloat16)
    factor_low = (factor_end - factor_high.astype(jnp.float32)).astype(jnp.bfloat16)
    row_slot = jnp.arange(16)[None, :, None]
    factor_rows = jnp.where(
        row_slot == 0,
        factor_high[:, None, None],
        jnp.where(row_slot == 1, factor_low[:, None, None], jnp.zeros((), jnp.bfloat16)),
    )
    factor_rows = jnp.broadcast_to(factor_rows, (local_heads, 16, state_size))
    packed = jnp.concatenate([zero_end.astype(jnp.bfloat16), factor_rows], axis=1)
    sent = lax.all_to_all(jnp.tile(packed[None], (seq_count, 1, 1, 1)), "seq", 0, 0, tiled=True)
    sent_states = sent[:, :, :head_size]
    sent_factors = sent[:, :, head_size, 0].astype(jnp.float32) + sent[
        :, :, head_size + 1, 0
    ].astype(jnp.float32)
    seq_index = lax.axis_index("seq")
    incoming = empty
    for earlier in range(seq_count - 1):
        advanced = sent_factors[earlier][:, None, None] * incoming + sent_states[earlier].astype(
            jnp.float32
        )
        incoming = jnp.where(earlier < seq_index, advanced, incoming)
    block_states = zero_starts + factors[:, :, None, None] * incoming[None]
    keep = jnp.exp(decay_sum) * (segs == prior[:, None]).astype(jnp.float32)[..., None]
    outer = keep[..., None] * jnp.einsum(
        "cin,chpn->cihp", queries, block_states, precision=HIGH_PRECISION
    )
    output = (inner + outer + skip_gain[None, None, :, None] * values).reshape(
        row_count, local_inner
    )
    gated = output * jax.nn.silu(gate)
    squares = jnp.sum(gated * gated, axis=1)
    unscaled = (gated * norm_gain[None, :]).astype(jnp.bfloat16)
    squares_high = squares.astype(jnp.bfloat16)
    squares_low = (squares - squares_high.astype(jnp.float32)).astype(jnp.bfloat16)
    column_slot = jnp.arange(128)[None, :]
    square_columns = jnp.where(
        column_slot == 0,
        squares_high[:, None],
        jnp.where(column_slot == 1, squares_low[:, None], jnp.zeros((), jnp.bfloat16)),
    )
    width = out_weight.shape[1]
    widened_weight = jnp.concatenate(
        [
            jnp.concatenate([out_weight, jnp.zeros((local_inner, 128), out_weight.dtype)], axis=1),
            jnp.concatenate(
                [jnp.zeros((128, width), out_weight.dtype), jnp.eye(128, dtype=out_weight.dtype)],
                axis=1,
            ),
        ],
        axis=0,
    )
    partials = jnp.dot(
        jnp.concatenate([unscaled, square_columns], axis=1),
        widened_weight,
        preferred_element_type=jnp.float32,
    ).astype(jnp.bfloat16)
    received_partials = lax.all_to_all(partials, "tensor", 0, 0, tiled=True).reshape(
        tensor_count, -1, width + 128
    )
    totals = jnp.sum(
        received_partials[:, :, width].astype(jnp.float32)
        + received_partials[:, :, width + 1].astype(jnp.float32),
        axis=0,
    )
    scale = lax.rsqrt(totals[:, None] / (local_inner * tensor_count) + 1e-05)
    mixed = jnp.sum(
        received_partials[:, :, :width].astype(jnp.float32) * scale[None], axis=0
    ).astype(jnp.bfloat16)
    request_count = lengths.shape[0]
    request_ids = jnp.arange(request_count, dtype=jnp.int32)
    slot_request = jnp.sum(
        (slots[None, :] == request_ids[:, None]).astype(jnp.int32) * request_ids[None, :], axis=1
    )
    ends = jnp.take(starts + lengths - 1 - DRAFTS + accepted, slot_request)
    present = (ends >= first) & (ends < first + row_count)
    local_end = jnp.clip(ends - first, 0, row_count - 1)
    which = local_end // BLOCK
    place = local_end % BLOCK
    positions = jnp.arange(BLOCK, dtype=jnp.int32)
    bracket = jnp.zeros((request_count, local_heads, head_size, state_size), jnp.float32)
    coefficient = jnp.zeros((request_count, local_heads), jnp.float32)
    for block in range(block_count):
        in_block = (which == block) & present
        end_sums = jnp.take(decay_sum[block], place, axis=0)
        valid = (
            in_block[:, None]
            & (positions[None, :] <= place[:, None])
            & (segs[block][None, :] == slot_request[:, None])
        )
        weight = jnp.where(
            valid[..., None],
            jnp.exp(jnp.minimum(end_sums[:, None, :] - decay_sum[block][None], 0.0))
            * steps[block][None],
            0.0,
        )
        bracket = bracket + jnp.einsum(
            "rjhp,jn->rhpn",
            weight[..., None] * values[block][None],
            keys[block],
            preferred_element_type=jnp.float32,
        )
        carried = jnp.where(
            (in_block & (prior[block] == slot_request))[:, None], jnp.exp(end_sums), 0.0
        )
        bracket = bracket + carried[:, :, None, None] * zero_starts[block][None]
        coefficient = coefficient + carried * factors[block][None]
    outgoing = bracket + coefficient[:, :, None, None] * incoming[None]
    chunks = outgoing.astype(jnp.bfloat16).reshape(
        seq_count, request_count // seq_count, local_heads, head_size, state_size
    )
    pieces = [jnp.take(chunks, seq_index, axis=0).astype(jnp.float32)]
    for distance in range(1, seq_count):
        target = (seq_index + distance) % seq_count
        route = [(i, (i + distance) % seq_count) for i in range(seq_count)]
        pieces.append(
            lax.ppermute(jnp.take(chunks, target, axis=0), "seq", route).astype(jnp.float32)
        )
    mine = sum(pieces[1:], pieces[0])
    return (mixed, mine)


def solution(mesh):
    return jax.shard_map(
        per_device,
        mesh=mesh,
        in_specs=(
            P(("seq", "tensor"), None),
            P(None, "tensor"),
            P(None, "tensor"),
            P(None, "tensor"),
            P(),
            P(None, "tensor"),
            P("tensor"),
            P(),
            P(),
            P("tensor"),
            P("tensor"),
            P("tensor"),
            P("tensor"),
            P("tensor", None),
            P(),
            P(),
            P(),
        ),
        out_specs=(P(("seq", "tensor"), None), P("seq", "tensor", None, None)),
        check_vma=False,
    )
```

```python
import jax
import jax.numpy as jnp
from jax import lax
from jax.sharding import PartitionSpec as P

BLOCK = 256
DRAFTS = 16


HIGHEST_PRECISION = lax.Precision.HIGHEST
HIGH_PRECISION = lax.Precision.HIGH


def passed_along(block, axis, distance):
    devices = range(lax.axis_size(axis))
    route = [(i - distance, i) for i in devices if i - distance in devices]
    return lax.ppermute(block, axis, route)


def segment_of(positions, starts):
    return jnp.sum((starts[None, :] <= positions[:, None]).astype(jnp.int32), axis=1) - 1


def per_device(
    tokens,
    in_gate,
    in_x,
    in_dt,
    in_bc,
    conv_x_weight,
    conv_x_bias,
    conv_bc_weight,
    conv_bc_bias,
    dt_bias,
    head_rate,
    skip_gain,
    norm_gain,
    out_weight,
    lengths,
    accepted,
    slots,
):
    local_inner = in_x.shape[1]
    local_heads = in_dt.shape[1]
    head_size = local_inner // local_heads
    state_size = in_bc.shape[1] // 2
    tensor_count = lax.axis_size("tensor")
    seq_count = lax.axis_size("seq")
    weight_all = jnp.concatenate([in_gate, in_x, in_dt, in_bc], axis=1)
    gathered = lax.all_to_all(
        jnp.tile(tokens, (lax.axis_size("tensor"), 1)), "tensor", 0, 0, tiled=True
    )
    projected = jnp.dot(
        gathered,
        weight_all,
        preferred_element_type=jnp.float32,
    )
    bc_inputs = projected[:, 2 * local_inner + local_heads :]
    gate = projected[:, :local_inner]
    raw_step = projected[:, 2 * local_inner : 2 * local_inner + local_heads]
    inputs = jnp.concatenate([projected[:, local_inner : 2 * local_inner], bc_inputs], axis=1)
    row_count = projected.shape[0]
    first = lax.axis_index("seq") * row_count
    starts = jnp.cumsum(lengths) - lengths
    segment = segment_of(first + jnp.arange(row_count, dtype=jnp.int32), starts)
    taps = conv_x_weight.shape[0]
    edge = passed_along(inputs[row_count - taps + 1 :], "seq", 1)
    edge_segment = segment_of(first - taps + 1 + jnp.arange(taps - 1, dtype=jnp.int32), starts)
    extended = jnp.concatenate([edge, inputs], axis=0)
    extended_segment = jnp.concatenate([edge_segment, segment])
    conv_weight = jnp.concatenate([conv_x_weight, conv_bc_weight], axis=1)
    conv_bias = jnp.concatenate([conv_x_bias, conv_bc_bias])
    conv = jnp.zeros_like(inputs) + conv_bias[None, :]
    for offset in range(taps):
        match = (extended_segment[offset : offset + row_count] == segment).astype(jnp.float32)
        conv = (
            conv
            + conv_weight[offset][None, :] * extended[offset : offset + row_count] * match[:, None]
        )
    active = jax.nn.silu(conv)
    block_count = row_count // BLOCK
    values = active[:, :local_inner].reshape(block_count, BLOCK, local_heads, head_size)
    keys = active[:, local_inner : local_inner + state_size].reshape(block_count, BLOCK, state_size)
    queries = active[:, local_inner + state_size :].reshape(block_count, BLOCK, state_size)
    step_size = jax.nn.softplus(raw_step + dt_bias[None, :])
    lower_ones = (
        jnp.arange(BLOCK)[:, None] >= jnp.arange(BLOCK)[None, :]
    ).astype(jnp.float32)
    decay_sum = jnp.einsum(
        "ij,cjh->cih",
        lower_ones,
        (-head_rate[None, :] * step_size).reshape(block_count, BLOCK, local_heads),
        precision=HIGHEST_PRECISION,
    )
    steps = step_size.reshape(block_count, BLOCK, local_heads)
    segs = segment.reshape(block_count, BLOCK)
    prior = segment_of(first + jnp.arange(block_count, dtype=jnp.int32) * BLOCK - 1, starts)
    lower = jnp.arange(BLOCK)[:, None] >= jnp.arange(BLOCK)[None, :]
    same = (segs[:, :, None] == segs[:, None, :]) & lower[None]
    spread = decay_sum[:, :, None, :] - decay_sum[:, None, :, :]
    decay = jnp.where(same[..., None], jnp.exp(jnp.minimum(spread, 0.0)), 0.0)
    gram = jnp.einsum("cin,cjn->cij", queries, keys, precision=HIGH_PRECISION)
    mixing = gram[..., None] * decay * steps[:, None, :, :]
    inner = jnp.einsum("cijh,cjhp->cihp", mixing, values, precision=HIGH_PRECISION)
    last_match = (segs == segs[:, -1:]).astype(jnp.float32)
    weight_last = jnp.exp(decay_sum[:, -1:, :] - decay_sum) * steps * last_match[..., None]
    local = jnp.einsum(
        "cjhp,cjn->chpn", weight_last[..., None] * values, keys, precision=HIGH_PRECISION
    )
    passes = jnp.exp(decay_sum[:, -1, :]) * (segs[:, -1] == prior).astype(jnp.float32)[:, None]

    empty = jnp.zeros((local_heads, head_size, state_size), jnp.float32)
    zero_start_list = []
    factor_list = []
    zero_end = empty
    factor_end = jnp.ones((local_heads,), jnp.float32)
    for block in range(block_count):
        zero_start_list.append(zero_end)
        factor_list.append(factor_end)
        zero_end = passes[block][:, None, None] * zero_end + local[block]
        factor_end = passes[block] * factor_end
    zero_starts = jnp.stack(zero_start_list)
    factors = jnp.stack(factor_list)

    factor_high = factor_end.astype(jnp.bfloat16)
    factor_low = (factor_end - factor_high.astype(jnp.float32)).astype(jnp.bfloat16)
    row_slot = jnp.arange(16)[None, :, None]
    factor_rows = jnp.where(
        row_slot == 0,
        factor_high[:, None, None],
        jnp.where(row_slot == 1, factor_low[:, None, None], jnp.zeros((), jnp.bfloat16)),
    )
    factor_rows = jnp.broadcast_to(factor_rows, (local_heads, 16, state_size))
    packed = jnp.concatenate([zero_end.astype(jnp.bfloat16), factor_rows], axis=1)
    seq_index = lax.axis_index("seq")
    incoming = empty
    for distance in range(seq_count - 1, 0, -1):
        route = [(i, i + distance) for i in range(seq_count - distance)]
        message = lax.ppermute(packed, "seq", route)
        message_factor = message[:, head_size, 0].astype(jnp.float32) + message[
            :, head_size + 1, 0
        ].astype(jnp.float32)
        advanced = message_factor[:, None, None] * incoming + message[:, :head_size].astype(
            jnp.float32
        )
        incoming = jnp.where(distance <= seq_index, advanced, incoming)
    block_states = zero_starts + factors[:, :, None, None] * incoming[None]
    keep = jnp.exp(decay_sum) * (segs == prior[:, None]).astype(jnp.float32)[..., None]
    outer = keep[..., None] * jnp.einsum(
        "cin,chpn->cihp", queries, block_states, precision=HIGH_PRECISION
    )
    output = (inner + outer + skip_gain[None, None, :, None] * values).reshape(
        row_count, local_inner
    )
    gated = output * jax.nn.silu(gate)
    squares = jnp.sum(gated * gated, axis=1)
    unscaled = (gated * norm_gain[None, :]).astype(jnp.bfloat16)
    squares_high = squares.astype(jnp.bfloat16)
    squares_low = (squares - squares_high.astype(jnp.float32)).astype(jnp.bfloat16)
    column_slot = jnp.arange(128)[None, :]
    square_columns = jnp.where(
        column_slot == 0,
        squares_high[:, None],
        jnp.where(column_slot == 1, squares_low[:, None], jnp.zeros((), jnp.bfloat16)),
    )
    width = out_weight.shape[1]
    widened_weight = jnp.concatenate(
        [
            jnp.concatenate([out_weight, jnp.zeros((local_inner, 128), out_weight.dtype)], axis=1),
            jnp.concatenate(
                [jnp.zeros((128, width), out_weight.dtype), jnp.eye(128, dtype=out_weight.dtype)],
                axis=1,
            ),
        ],
        axis=0,
    )
    partials = jnp.dot(
        jnp.concatenate([unscaled, square_columns], axis=1),
        widened_weight,
        preferred_element_type=jnp.float32,
    ).astype(jnp.bfloat16)
    received_partials = lax.all_to_all(partials, "tensor", 0, 0, tiled=True).reshape(
        tensor_count, -1, width + 128
    )
    totals = jnp.sum(
        received_partials[:, :, width].astype(jnp.float32)
        + received_partials[:, :, width + 1].astype(jnp.float32),
        axis=0,
    )
    scale = lax.rsqrt(totals[:, None] / (local_inner * tensor_count) + 1e-05)
    mixed = jnp.sum(
        received_partials[:, :, :width].astype(jnp.float32) * scale[None], axis=0
    ).astype(jnp.bfloat16)
    request_count = lengths.shape[0]
    request_ids = jnp.arange(request_count, dtype=jnp.int32)
    slot_request = jnp.sum(
        (slots[None, :] == request_ids[:, None]).astype(jnp.int32) * request_ids[None, :], axis=1
    )
    ends = jnp.take(starts + lengths - 1 - DRAFTS + accepted, slot_request)
    present = (ends >= first) & (ends < first + row_count)
    local_end = jnp.clip(ends - first, 0, row_count - 1)
    which = local_end // BLOCK
    place = local_end % BLOCK
    positions = jnp.arange(BLOCK, dtype=jnp.int32)
    bracket = jnp.zeros((request_count, local_heads, head_size, state_size), jnp.float32)
    coefficient = jnp.zeros((request_count, local_heads), jnp.float32)
    for block in range(block_count):
        in_block = (which == block) & present
        end_sums = jnp.take(decay_sum[block], place, axis=0)
        valid = (
            in_block[:, None]
            & (positions[None, :] <= place[:, None])
            & (segs[block][None, :] == slot_request[:, None])
        )
        weight = jnp.where(
            valid[..., None],
            jnp.exp(jnp.minimum(end_sums[:, None, :] - decay_sum[block][None], 0.0))
            * steps[block][None],
            0.0,
        )
        bracket = bracket + jnp.einsum(
            "rjhp,jn->rhpn",
            weight[..., None] * values[block][None],
            keys[block],
            preferred_element_type=jnp.float32,
        )
        carried = jnp.where(
            (in_block & (prior[block] == slot_request))[:, None], jnp.exp(end_sums), 0.0
        )
        bracket = bracket + carried[:, :, None, None] * zero_starts[block][None]
        coefficient = coefficient + carried * factors[block][None]
    outgoing = bracket + coefficient[:, :, None, None] * incoming[None]
    chunks = outgoing.astype(jnp.bfloat16).reshape(
        seq_count, request_count // seq_count, local_heads, head_size, state_size
    )
    pieces = [jnp.take(chunks, seq_index, axis=0).astype(jnp.float32)]
    for distance in range(1, seq_count):
        target = (seq_index + distance) % seq_count
        route = [(i, (i + distance) % seq_count) for i in range(seq_count)]
        pieces.append(
            lax.ppermute(jnp.take(chunks, target, axis=0), "seq", route).astype(jnp.float32)
        )
    mine = sum(pieces[1:], pieces[0])
    return (mixed, mine)


def solution(mesh):
    return jax.shard_map(
        per_device,
        mesh=mesh,
        in_specs=(
            P(("seq", "tensor"), None),
            P(None, "tensor"),
            P(None, "tensor"),
            P(None, "tensor"),
            P(),
            P(None, "tensor"),
            P("tensor"),
            P(),
            P(),
            P("tensor"),
            P("tensor"),
            P("tensor"),
            P("tensor"),
            P("tensor", None),
            P(),
            P(),
            P(),
        ),
        out_specs=(P(("seq", "tensor"), None), P("seq", "tensor", None, None)),
        check_vma=False,
    )
```

```python
import jax
import jax.numpy as jnp
from jax import lax
from jax.sharding import PartitionSpec as P

BLOCK = 256
DRAFTS = 16


HIGHEST_PRECISION = lax.Precision.HIGHEST
HIGH_PRECISION = lax.Precision.HIGH


def passed_along(block, axis, distance):
    devices = range(lax.axis_size(axis))
    route = [(i - distance, i) for i in devices if i - distance in devices]
    return lax.ppermute(block, axis, route)


def segment_of(positions, starts):
    return jnp.sum((starts[None, :] <= positions[:, None]).astype(jnp.int32), axis=1) - 1


def per_device(
    tokens,
    in_gate,
    in_x,
    in_dt,
    in_bc,
    conv_x_weight,
    conv_x_bias,
    conv_bc_weight,
    conv_bc_bias,
    dt_bias,
    head_rate,
    skip_gain,
    norm_gain,
    out_weight,
    lengths,
    accepted,
    slots,
):
    local_inner = in_x.shape[1]
    local_heads = in_dt.shape[1]
    head_size = local_inner // local_heads
    state_size = in_bc.shape[1] // 2
    tensor_count = lax.axis_size("tensor")
    seq_count = lax.axis_size("seq")
    weight_all = jnp.concatenate([in_gate, in_x, in_dt, in_bc], axis=1)
    gathered = lax.all_to_all(
        jnp.tile(tokens, (lax.axis_size("tensor"), 1)), "tensor", 0, 0, tiled=True
    )
    projected = jnp.dot(
        gathered,
        weight_all,
        preferred_element_type=jnp.float32,
    )
    bc_inputs = projected[:, 2 * local_inner + local_heads :]
    gate = projected[:, :local_inner]
    raw_step = projected[:, 2 * local_inner : 2 * local_inner + local_heads]
    inputs = jnp.concatenate([projected[:, local_inner : 2 * local_inner], bc_inputs], axis=1)
    row_count = projected.shape[0]
    first = lax.axis_index("seq") * row_count
    starts = jnp.cumsum(lengths) - lengths
    segment = segment_of(first + jnp.arange(row_count, dtype=jnp.int32), starts)
    taps = conv_x_weight.shape[0]
    edge = passed_along(inputs[row_count - taps + 1 :], "seq", 1)
    edge_segment = segment_of(first - taps + 1 + jnp.arange(taps - 1, dtype=jnp.int32), starts)
    extended = jnp.concatenate([edge, inputs], axis=0)
    extended_segment = jnp.concatenate([edge_segment, segment])
    conv_weight = jnp.concatenate([conv_x_weight, conv_bc_weight], axis=1)
    conv_bias = jnp.concatenate([conv_x_bias, conv_bc_bias])
    conv = jnp.zeros_like(inputs) + conv_bias[None, :]
    for offset in range(taps):
        match = (extended_segment[offset : offset + row_count] == segment).astype(jnp.float32)
        conv = (
            conv
            + conv_weight[offset][None, :] * extended[offset : offset + row_count] * match[:, None]
        )
    active = jax.nn.silu(conv)
    block_count = row_count // BLOCK
    values = active[:, :local_inner].reshape(block_count, BLOCK, local_heads, head_size)
    keys = active[:, local_inner : local_inner + state_size].reshape(block_count, BLOCK, state_size)
    queries = active[:, local_inner + state_size :].reshape(block_count, BLOCK, state_size)
    step_size = jax.nn.softplus(raw_step + dt_bias[None, :])
    lower_ones = (
        jnp.arange(BLOCK)[:, None] >= jnp.arange(BLOCK)[None, :]
    ).astype(jnp.float32)
    decay_sum = jnp.einsum(
        "ij,cjh->cih",
        lower_ones,
        (-head_rate[None, :] * step_size).reshape(block_count, BLOCK, local_heads),
        precision=HIGHEST_PRECISION,
    )
    steps = step_size.reshape(block_count, BLOCK, local_heads)
    segs = segment.reshape(block_count, BLOCK)
    prior = segment_of(first + jnp.arange(block_count, dtype=jnp.int32) * BLOCK - 1, starts)
    lower = jnp.arange(BLOCK)[:, None] >= jnp.arange(BLOCK)[None, :]
    same = (segs[:, :, None] == segs[:, None, :]) & lower[None]
    spread = decay_sum[:, :, None, :] - decay_sum[:, None, :, :]
    decay = jnp.where(same[..., None], jnp.exp(jnp.minimum(spread, 0.0)), 0.0)
    gram = jnp.einsum("cin,cjn->cij", queries, keys, precision=HIGH_PRECISION)
    mixing = gram[..., None] * decay * steps[:, None, :, :]
    inner = jnp.einsum("cijh,cjhp->cihp", mixing, values, precision=HIGH_PRECISION)
    last_match = (segs == segs[:, -1:]).astype(jnp.float32)
    weight_last = jnp.exp(decay_sum[:, -1:, :] - decay_sum) * steps * last_match[..., None]
    local = jnp.einsum(
        "cjhp,cjn->chpn", weight_last[..., None] * values, keys, precision=HIGH_PRECISION
    )
    passes = jnp.exp(decay_sum[:, -1, :]) * (segs[:, -1] == prior).astype(jnp.float32)[:, None]

    empty = jnp.zeros((local_heads, head_size, state_size), jnp.float32)
    zero_start_list = []
    factor_list = []
    zero_end = empty
    factor_end = jnp.ones((local_heads,), jnp.float32)
    for block in range(block_count):
        zero_start_list.append(zero_end)
        factor_list.append(factor_end)
        zero_end = passes[block][:, None, None] * zero_end + local[block]
        factor_end = passes[block] * factor_end
    zero_starts = jnp.stack(zero_start_list)
    factors = jnp.stack(factor_list)

    factor_high = factor_end.astype(jnp.bfloat16)
    factor_low = (factor_end - factor_high.astype(jnp.float32)).astype(jnp.bfloat16)
    row_slot = jnp.arange(16)[None, :, None]
    factor_rows = jnp.where(
        row_slot == 0,
        factor_high[:, None, None],
        jnp.where(row_slot == 1, factor_low[:, None, None], jnp.zeros((), jnp.bfloat16)),
    )
    factor_rows = jnp.broadcast_to(factor_rows, (local_heads, 16, state_size))
    packed = jnp.concatenate([zero_end.astype(jnp.bfloat16), factor_rows], axis=1)
    sent = lax.all_gather(packed, "seq", axis=0)
    sent_states = sent[:, :, :head_size]
    sent_factors = sent[:, :, head_size, 0].astype(jnp.float32) + sent[
        :, :, head_size + 1, 0
    ].astype(jnp.float32)
    seq_index = lax.axis_index("seq")
    incoming = empty
    for earlier in range(seq_count - 1):
        advanced = sent_factors[earlier][:, None, None] * incoming + sent_states[earlier].astype(
            jnp.float32
        )
        incoming = jnp.where(earlier < seq_index, advanced, incoming)
    block_states = zero_starts + factors[:, :, None, None] * incoming[None]
    keep = jnp.exp(decay_sum) * (segs == prior[:, None]).astype(jnp.float32)[..., None]
    outer = keep[..., None] * jnp.einsum(
        "cin,chpn->cihp", queries, block_states, precision=HIGH_PRECISION
    )
    output = (inner + outer + skip_gain[None, None, :, None] * values).reshape(
        row_count, local_inner
    )
    gated = output * jax.nn.silu(gate)
    squares = jnp.sum(gated * gated, axis=1)
    unscaled = (gated * norm_gain[None, :]).astype(jnp.bfloat16)
    squares_high = squares.astype(jnp.bfloat16)
    squares_low = (squares - squares_high.astype(jnp.float32)).astype(jnp.bfloat16)
    column_slot = jnp.arange(128)[None, :]
    square_columns = jnp.where(
        column_slot == 0,
        squares_high[:, None],
        jnp.where(column_slot == 1, squares_low[:, None], jnp.zeros((), jnp.bfloat16)),
    )
    width = out_weight.shape[1]
    widened_weight = jnp.concatenate(
        [
            jnp.concatenate([out_weight, jnp.zeros((local_inner, 128), out_weight.dtype)], axis=1),
            jnp.concatenate(
                [jnp.zeros((128, width), out_weight.dtype), jnp.eye(128, dtype=out_weight.dtype)],
                axis=1,
            ),
        ],
        axis=0,
    )
    partials = jnp.dot(
        jnp.concatenate([unscaled, square_columns], axis=1),
        widened_weight,
        preferred_element_type=jnp.float32,
    ).astype(jnp.bfloat16)
    received_partials = lax.all_to_all(partials, "tensor", 0, 0, tiled=True).reshape(
        tensor_count, -1, width + 128
    )
    totals = jnp.sum(
        received_partials[:, :, width].astype(jnp.float32)
        + received_partials[:, :, width + 1].astype(jnp.float32),
        axis=0,
    )
    scale = lax.rsqrt(totals[:, None] / (local_inner * tensor_count) + 1e-05)
    mixed = jnp.sum(
        received_partials[:, :, :width].astype(jnp.float32) * scale[None], axis=0
    ).astype(jnp.bfloat16)
    request_count = lengths.shape[0]
    request_ids = jnp.arange(request_count, dtype=jnp.int32)
    slot_request = jnp.sum(
        (slots[None, :] == request_ids[:, None]).astype(jnp.int32) * request_ids[None, :], axis=1
    )
    ends = jnp.take(starts + lengths - 1 - DRAFTS + accepted, slot_request)
    present = (ends >= first) & (ends < first + row_count)
    local_end = jnp.clip(ends - first, 0, row_count - 1)
    which = local_end // BLOCK
    place = local_end % BLOCK
    positions = jnp.arange(BLOCK, dtype=jnp.int32)
    bracket = jnp.zeros((request_count, local_heads, head_size, state_size), jnp.float32)
    coefficient = jnp.zeros((request_count, local_heads), jnp.float32)
    for block in range(block_count):
        in_block = (which == block) & present
        end_sums = jnp.take(decay_sum[block], place, axis=0)
        valid = (
            in_block[:, None]
            & (positions[None, :] <= place[:, None])
            & (segs[block][None, :] == slot_request[:, None])
        )
        weight = jnp.where(
            valid[..., None],
            jnp.exp(jnp.minimum(end_sums[:, None, :] - decay_sum[block][None], 0.0))
            * steps[block][None],
            0.0,
        )
        bracket = bracket + jnp.einsum(
            "rjhp,jn->rhpn",
            weight[..., None] * values[block][None],
            keys[block],
            preferred_element_type=jnp.float32,
        )
        carried = jnp.where(
            (in_block & (prior[block] == slot_request))[:, None], jnp.exp(end_sums), 0.0
        )
        bracket = bracket + carried[:, :, None, None] * zero_starts[block][None]
        coefficient = coefficient + carried * factors[block][None]
    outgoing = bracket + coefficient[:, :, None, None] * incoming[None]
    chunks = outgoing.astype(jnp.bfloat16).reshape(
        seq_count, request_count // seq_count, local_heads, head_size, state_size
    )
    pieces = [jnp.take(chunks, seq_index, axis=0).astype(jnp.float32)]
    for distance in range(1, seq_count):
        target = (seq_index + distance) % seq_count
        route = [(i, (i + distance) % seq_count) for i in range(seq_count)]
        pieces.append(
            lax.ppermute(jnp.take(chunks, target, axis=0), "seq", route).astype(jnp.float32)
        )
    mine = sum(pieces[1:], pieces[0])
    return (mixed, mine)


def solution(mesh):
    return jax.shard_map(
        per_device,
        mesh=mesh,
        in_specs=(
            P(("seq", "tensor"), None),
            P(None, "tensor"),
            P(None, "tensor"),
            P(None, "tensor"),
            P(),
            P(None, "tensor"),
            P("tensor"),
            P(),
            P(),
            P("tensor"),
            P("tensor"),
            P("tensor"),
            P("tensor"),
            P("tensor", None),
            P(),
            P(),
            P(),
        ),
        out_specs=(P(("seq", "tensor"), None), P("seq", "tensor", None, None)),
        check_vma=False,
    )
```

```python
import jax
import jax.numpy as jnp
from jax import lax
from jax.sharding import PartitionSpec as P

BLOCK = 256
DRAFTS = 16


HIGHEST_PRECISION = lax.Precision.HIGHEST
HIGH_PRECISION = lax.Precision.HIGH


def passed_along(block, axis, distance):
    devices = range(lax.axis_size(axis))
    route = [(i - distance, i) for i in devices if i - distance in devices]
    return lax.ppermute(block, axis, route)


def segment_of(positions, starts):
    return jnp.sum((starts[None, :] <= positions[:, None]).astype(jnp.int32), axis=1) - 1


def per_device(
    tokens,
    in_gate,
    in_x,
    in_dt,
    in_bc,
    conv_x_weight,
    conv_x_bias,
    conv_bc_weight,
    conv_bc_bias,
    dt_bias,
    head_rate,
    skip_gain,
    norm_gain,
    out_weight,
    lengths,
    accepted,
    slots,
):
    local_inner = in_x.shape[1]
    local_heads = in_dt.shape[1]
    head_size = local_inner // local_heads
    state_size = in_bc.shape[1] // 2
    tensor_count = lax.axis_size("tensor")
    seq_count = lax.axis_size("seq")
    weight_all = jnp.concatenate([in_gate, in_x, in_dt, in_bc], axis=1)
    gathered = lax.all_to_all(
        jnp.tile(tokens, (lax.axis_size("tensor"), 1)), "tensor", 0, 0, tiled=True
    )
    projected = jnp.dot(
        gathered,
        weight_all,
        preferred_element_type=jnp.float32,
    )
    bc_inputs = projected[:, 2 * local_inner + local_heads :]
    gate = projected[:, :local_inner]
    raw_step = projected[:, 2 * local_inner : 2 * local_inner + local_heads]
    inputs = jnp.concatenate([projected[:, local_inner : 2 * local_inner], bc_inputs], axis=1)
    row_count = projected.shape[0]
    first = lax.axis_index("seq") * row_count
    starts = jnp.cumsum(lengths) - lengths
    segment = segment_of(first + jnp.arange(row_count, dtype=jnp.int32), starts)
    taps = conv_x_weight.shape[0]
    edge = passed_along(inputs[row_count - taps + 1 :], "seq", 1)
    edge_segment = segment_of(first - taps + 1 + jnp.arange(taps - 1, dtype=jnp.int32), starts)
    extended = jnp.concatenate([edge, inputs], axis=0)
    extended_segment = jnp.concatenate([edge_segment, segment])
    conv_weight = jnp.concatenate([conv_x_weight, conv_bc_weight], axis=1)
    conv_bias = jnp.concatenate([conv_x_bias, conv_bc_bias])
    conv = jnp.zeros_like(inputs) + conv_bias[None, :]
    for offset in range(taps):
        match = (extended_segment[offset : offset + row_count] == segment).astype(jnp.float32)
        conv = (
            conv
            + conv_weight[offset][None, :] * extended[offset : offset + row_count] * match[:, None]
        )
    active = jax.nn.silu(conv)
    block_count = row_count // BLOCK
    values = active[:, :local_inner].reshape(block_count, BLOCK, local_heads, head_size)
    keys = active[:, local_inner : local_inner + state_size].reshape(block_count, BLOCK, state_size)
    queries = active[:, local_inner + state_size :].reshape(block_count, BLOCK, state_size)
    step_size = jax.nn.softplus(raw_step + dt_bias[None, :])
    lower_ones = (
        jnp.arange(BLOCK)[:, None] >= jnp.arange(BLOCK)[None, :]
    ).astype(jnp.float32)
    decay_sum = jnp.einsum(
        "ij,cjh->cih",
        lower_ones,
        (-head_rate[None, :] * step_size).reshape(block_count, BLOCK, local_heads),
        precision=HIGHEST_PRECISION,
    )
    steps = step_size.reshape(block_count, BLOCK, local_heads)
    segs = segment.reshape(block_count, BLOCK)
    prior = segment_of(first + jnp.arange(block_count, dtype=jnp.int32) * BLOCK - 1, starts)
    lower = jnp.arange(BLOCK)[:, None] >= jnp.arange(BLOCK)[None, :]
    same = (segs[:, :, None] == segs[:, None, :]) & lower[None]
    spread = decay_sum[:, :, None, :] - decay_sum[:, None, :, :]
    decay = jnp.where(same[..., None], jnp.exp(jnp.minimum(spread, 0.0)), 0.0)
    gram = jnp.einsum("cin,cjn->cij", queries, keys, precision=HIGH_PRECISION)
    mixing = gram[..., None] * decay * steps[:, None, :, :]
    inner = jnp.einsum("cijh,cjhp->cihp", mixing, values, precision=HIGH_PRECISION)
    last_match = (segs == segs[:, -1:]).astype(jnp.float32)
    weight_last = jnp.exp(decay_sum[:, -1:, :] - decay_sum) * steps * last_match[..., None]
    local = jnp.einsum(
        "cjhp,cjn->chpn", weight_last[..., None] * values, keys, preferred_element_type=jnp.float32
    )
    passes = jnp.exp(decay_sum[:, -1, :]) * (segs[:, -1] == prior).astype(jnp.float32)[:, None]

    empty = jnp.zeros((local_heads, head_size, state_size), jnp.float32)
    zero_start_list = []
    factor_list = []
    zero_end = empty
    factor_end = jnp.ones((local_heads,), jnp.float32)
    for block in range(block_count):
        zero_start_list.append(zero_end)
        factor_list.append(factor_end)
        zero_end = passes[block][:, None, None] * zero_end + local[block]
        factor_end = passes[block] * factor_end
    zero_starts = jnp.stack(zero_start_list)
    factors = jnp.stack(factor_list)

    factor_high = factor_end.astype(jnp.bfloat16)
    factor_low = (factor_end - factor_high.astype(jnp.float32)).astype(jnp.bfloat16)
    row_slot = jnp.arange(16)[None, :, None]
    factor_rows = jnp.where(
        row_slot == 0,
        factor_high[:, None, None],
        jnp.where(row_slot == 1, factor_low[:, None, None], jnp.zeros((), jnp.bfloat16)),
    )
    factor_rows = jnp.broadcast_to(factor_rows, (local_heads, 16, state_size))
    packed = jnp.concatenate([zero_end.astype(jnp.bfloat16), factor_rows], axis=1)
    sent = lax.all_to_all(jnp.tile(packed[None], (seq_count, 1, 1, 1)), "seq", 0, 0, tiled=True)
    sent_states = sent[:, :, :head_size]
    sent_factors = sent[:, :, head_size, 0].astype(jnp.float32) + sent[
        :, :, head_size + 1, 0
    ].astype(jnp.float32)
    seq_index = lax.axis_index("seq")
    incoming = empty
    for earlier in range(seq_count - 1):
        advanced = sent_factors[earlier][:, None, None] * incoming + sent_states[earlier].astype(
            jnp.float32
        )
        incoming = jnp.where(earlier < seq_index, advanced, incoming)
    block_states = zero_starts + factors[:, :, None, None] * incoming[None]
    keep = jnp.exp(decay_sum) * (segs == prior[:, None]).astype(jnp.float32)[..., None]
    outer = keep[..., None] * jnp.einsum(
        "cin,chpn->cihp", queries, block_states, preferred_element_type=jnp.float32
    )
    output = (inner + outer + skip_gain[None, None, :, None] * values).reshape(
        row_count, local_inner
    )
    gated = output * jax.nn.silu(gate)
    squares = jnp.sum(gated * gated, axis=1)
    unscaled = (gated * norm_gain[None, :]).astype(jnp.bfloat16)
    squares_high = squares.astype(jnp.bfloat16)
    squares_low = (squares - squares_high.astype(jnp.float32)).astype(jnp.bfloat16)
    column_slot = jnp.arange(128)[None, :]
    square_columns = jnp.where(
        column_slot == 0,
        squares_high[:, None],
        jnp.where(column_slot == 1, squares_low[:, None], jnp.zeros((), jnp.bfloat16)),
    )
    width = out_weight.shape[1]
    widened_weight = jnp.concatenate(
        [
            jnp.concatenate([out_weight, jnp.zeros((local_inner, 128), out_weight.dtype)], axis=1),
            jnp.concatenate(
                [jnp.zeros((128, width), out_weight.dtype), jnp.eye(128, dtype=out_weight.dtype)],
                axis=1,
            ),
        ],
        axis=0,
    )
    partials = jnp.dot(
        jnp.concatenate([unscaled, square_columns], axis=1),
        widened_weight,
        preferred_element_type=jnp.float32,
    ).astype(jnp.bfloat16)
    received_partials = lax.all_to_all(partials, "tensor", 0, 0, tiled=True).reshape(
        tensor_count, -1, width + 128
    )
    totals = jnp.sum(
        received_partials[:, :, width].astype(jnp.float32)
        + received_partials[:, :, width + 1].astype(jnp.float32),
        axis=0,
    )
    scale = lax.rsqrt(totals[:, None] / (local_inner * tensor_count) + 1e-05)
    mixed = jnp.sum(
        received_partials[:, :, :width].astype(jnp.float32) * scale[None], axis=0
    ).astype(jnp.bfloat16)
    request_count = lengths.shape[0]
    request_ids = jnp.arange(request_count, dtype=jnp.int32)
    slot_request = jnp.sum(
        (slots[None, :] == request_ids[:, None]).astype(jnp.int32) * request_ids[None, :], axis=1
    )
    ends = jnp.take(starts + lengths - 1 - DRAFTS + accepted, slot_request)
    present = (ends >= first) & (ends < first + row_count)
    local_end = jnp.clip(ends - first, 0, row_count - 1)
    which = local_end // BLOCK
    place = local_end % BLOCK
    positions = jnp.arange(BLOCK, dtype=jnp.int32)
    bracket = jnp.zeros((request_count, local_heads, head_size, state_size), jnp.float32)
    coefficient = jnp.zeros((request_count, local_heads), jnp.float32)
    for block in range(block_count):
        in_block = (which == block) & present
        end_sums = jnp.take(decay_sum[block], place, axis=0)
        valid = (
            in_block[:, None]
            & (positions[None, :] <= place[:, None])
            & (segs[block][None, :] == slot_request[:, None])
        )
        weight = jnp.where(
            valid[..., None],
            jnp.exp(jnp.minimum(end_sums[:, None, :] - decay_sum[block][None], 0.0))
            * steps[block][None],
            0.0,
        )
        bracket = bracket + jnp.einsum(
            "rjhp,jn->rhpn",
            weight[..., None] * values[block][None],
            keys[block],
            preferred_element_type=jnp.float32,
        )
        carried = jnp.where(
            (in_block & (prior[block] == slot_request))[:, None], jnp.exp(end_sums), 0.0
        )
        bracket = bracket + carried[:, :, None, None] * zero_starts[block][None]
        coefficient = coefficient + carried * factors[block][None]
    outgoing = bracket + coefficient[:, :, None, None] * incoming[None]
    chunks = outgoing.astype(jnp.bfloat16).reshape(
        seq_count, request_count // seq_count, local_heads, head_size, state_size
    )
    pieces = [jnp.take(chunks, seq_index, axis=0).astype(jnp.float32)]
    for distance in range(1, seq_count):
        target = (seq_index + distance) % seq_count
        route = [(i, (i + distance) % seq_count) for i in range(seq_count)]
        pieces.append(
            lax.ppermute(jnp.take(chunks, target, axis=0), "seq", route).astype(jnp.float32)
        )
    mine = sum(pieces[1:], pieces[0])
    return (mixed, mine)


def solution(mesh):
    return jax.shard_map(
        per_device,
        mesh=mesh,
        in_specs=(
            P(("seq", "tensor"), None),
            P(None, "tensor"),
            P(None, "tensor"),
            P(None, "tensor"),
            P(),
            P(None, "tensor"),
            P("tensor"),
            P(),
            P(),
            P("tensor"),
            P("tensor"),
            P("tensor"),
            P("tensor"),
            P("tensor", None),
            P(),
            P(),
            P(),
        ),
        out_specs=(P(("seq", "tensor"), None), P("seq", "tensor", None, None)),
        check_vma=False,
    )
```
